32 devices in a mesh: dp: 8 (over y, x, core), expert: 4 (over z).
Axes of the slice: x: 2, y: 2, z: 4, core: 2. Of those that a mesh axis runs over, the one named last changes fastest.
Arguments:
- tokens: bfloat16 [4096, 1024], P(('dp', 'expert')), may hold values from -6 to 6
- expert_ids: int32 [4096, 2], P(('dp', 'expert')), may hold values from 0 to 3, all different within a row; in each aligned block of 128 rows (0 to 127, 128 to 255, ...) at most 96 rows name the same one
- routing: float32 [4096, 2], P(('dp', 'expert')), may hold values from 0.2 to 1
- w_gate: bfloat16 [4, 1024, 384], P('expert', 'dp'), may hold values from -0.1875 to 0.1875
- w_up: bfloat16 [4, 1024, 384], P('expert', 'dp'), may hold values from -0.1875 to 0.1875
- w_down: bfloat16 [4, 1024, 384], P('expert', 'dp'), may hold values from -0.3125 to 0.3125
- grad_out: bfloat16 [4096, 1024], P(('dp', 'expert')), may hold values from -6 to 6
Outputs:
- output: bfloat16 [4096, 1024], P(('dp', 'expert'))
- token_grad: bfloat16 [4096, 1024], P(('dp', 'expert'))
- down_grad: float32 [4, 1024, 384], P('expert', 'dp')
The draws below stay inside these ranges and needn't reach their ends.
Inputs may be any that keep to these rules, and one draw needn't show every extreme that they name: `expert_ids`: the 2 experts of a token differ. Among the 128 tokens of one device no expert is named by more than 96 (token, choice) pairs, and in every draw some device names some expert exactly 96 times.
All inputs are finite; a program needn't handle non-finite values.
Results may differ from the reference program's by a relative error of at most 0.0065.
Values may be sent and summed in bfloat16 or wider, within the bound.
No kernel may reach another device: no remote copies, remote signals or barrier semaphores. Data moves between devices by JAX's collectives and lax.ppermute only.
A program may use at most 64 MiB of HBM per device.

```python
import math
import jax
import jax.numpy as jnp
import numpy as np
from jax import lax

D = 1024
FF = 384
TOP = 2
TOK_DEV = 128
EXPERTS = 4
CAP = 96
TOKENS = 4096
N_DP = 8
N_EXPERT = 4


def levels(rng, extent, split, least, high):
    def one(position, blocks):
        draws = jax.random.uniform(jax.random.fold_in(jax.random.fold_in(rng, 6), position), (blocks,), jnp.float32, least / len(split), high / len(split))
        return jnp.repeat(jnp.exp(draws), extent[position] // blocks).reshape((-1,) + (1,) * (len(extent) - position - 1))

    factor_of = one(*split[0])
    for cut in split[1:]:
        factor_of = factor_of * one(*cut)
    return factor_of


def routed_block(key, own, number, rows, count, top, limit, skew):
    sequence = jax.random.permutation(key, count)
    crowded, common = shares(count, rows * top, limit, skew, True), shares(count, rows * top, limit, skew, False)
    places = jnp.arange(count)

    def named(lengths, offset_by):
        used = int((lengths > 0).sum())
        fixed = max(1, used // 4)
        shifted = fixed + (places - fixed + offset_by * (used - fixed)) % max(1, count - fixed)
        return jnp.zeros((count,), jnp.int32).at[sequence[jnp.where(places < fixed, places, shifted)]].set(jnp.asarray(lengths, jnp.int32))

    lengths = jnp.where(number % 4 == 0, named(crowded, number // 4), named(common, number - number // 4 - 1))
    mixed = jax.random.permutation(jax.random.fold_in(own, 3), count)
    giver, sink = mixed[0:count // 2 * 2:2], mixed[1:count // 2 * 2:2]
    slack = jnp.minimum(lengths[giver] - 1, limit - lengths[sink]) // 2
    slack = jnp.where((giver == sequence[0]) | (sink == sequence[0]) | (lengths[sink] == 0), 0, jnp.maximum(slack, 0))
    shifted = jax.random.randint(jax.random.fold_in(own, 4), (count // 2,), 0, 1 << 20) % (slack + 1)
    lengths = lengths.at[giver].add(-shifted).at[sink].add(shifted)
    labels = jnp.searchsorted(jnp.cumsum(lengths), jnp.arange(rows * top), side="right").astype(jnp.int32)
    table = labels.reshape(top, rows).T
    table = table[jax.random.permutation(jax.random.fold_in(own, 1), rows)]
    offset_by = jax.random.randint(jax.random.fold_in(own, 2), (rows, 1), 0, top)
    return jnp.take_along_axis(table, (jnp.arange(top)[None, :] + offset_by) % top, axis=1)


def shares(amount, total, limit, skew, full):
    loads = [(1 << 20) // math.isqrt(grade ** skew) + 1 for grade in range(1, amount + 1)]
    largest = limit if full else min(limit, max(-(-total // amount), total * loads[0] // sum(loads)))
    least = 1 if total - largest >= amount - 1 else 0
    holding, spare = [largest] + [least] * (amount - 1), total - largest - least * (amount - 1)
    while spare > 0:
        movable = [i for i in range(1, amount) if holding[i] < largest] or [i for i in range(1, amount) if holding[i] < limit]
        pool, left = sum([loads[i] for i in movable]), spare
        for i in movable:
            addition = min(limit - holding[i], max(1, left * loads[i] // pool), spare)
            holding[i] = holding[i] + addition
            spare = spare - addition
    return np.array(holding)


def bell_draw(rng, shape, scale, limit, cuts=(), held_as=jnp.bfloat16):
    drawn = scale * jax.random.normal(rng, shape, jnp.float32)
    if cuts:
        drawn = drawn * levels(rng, shape, cuts, -0.22, 0.18)
    return jnp.clip(drawn, -limit, limit).astype(held_as)


def setup_inputs(seed: int = 0) -> dict:
    keys = jax.random.split(jax.random.key(seed), 8)
    tokens = bell_draw(keys[0], (TOKENS, D), 1.0, 6.0, ((0, 32),))
    expert_ids_keys = jax.random.split(jax.random.fold_in(keys[1], 1), TOKENS // TOK_DEV)
    expert_ids_turns = jax.random.permutation(jax.random.fold_in(keys[1], 3), TOKENS // TOK_DEV)
    expert_ids = jax.vmap(lambda own, number: routed_block(jax.random.fold_in(keys[1], 2), own, number, TOK_DEV, EXPERTS, TOP, CAP, 2))(expert_ids_keys, expert_ids_turns).reshape((TOKENS, TOP))
    routing = jnp.clip(0.2 + 0.8 * jax.random.uniform(keys[2], (TOKENS, TOP), jnp.float32) ** levels(keys[2], (TOKENS, TOP), ((0, 32),), -0.2, 0.2), 0.2, 1.0)
    w_gate = bell_draw(keys[3], (EXPERTS, D, FF), D ** -0.5, 0.1875, ((0, 4), (1, 8)))
    w_up = bell_draw(keys[4], (EXPERTS, D, FF), D ** -0.5, 0.1875, ((0, 4), (1, 8)))
    w_down = bell_draw(keys[5], (EXPERTS, D, FF), FF ** -0.5, 0.3125, ((0, 4), (1, 8)))
    grad_out = bell_draw(keys[6], (TOKENS, D), 1.0, 6.0, ((0, 32),))
    return {"tokens": tokens, "expert_ids": expert_ids, "routing": routing, "w_gate": w_gate, "w_up": w_up, "w_down": w_down, "grad_out": grad_out}


def forward_rows(row_data, gate_w, up_w, down_w):
    gate_pre = jnp.dot(row_data.astype(jnp.float32), gate_w.astype(jnp.float32))
    up_pre = jnp.dot(row_data.astype(jnp.float32), up_w.astype(jnp.float32))
    sigmoid_val = jax.nn.sigmoid(gate_pre)
    hidden = (gate_pre * sigmoid_val * up_pre).astype(jnp.bfloat16)
    expert_out = jnp.dot(hidden.astype(jnp.float32), down_w.astype(jnp.float32).T).astype(jnp.bfloat16)
    return gate_pre, up_pre, hidden, expert_out


def backward_rows(grad_rows, gate_pre, up_pre, gate_w, up_w, down_w):
    hidden_grad = jnp.dot(grad_rows.astype(jnp.float32), down_w.astype(jnp.float32))
    sigmoid_val = jax.nn.sigmoid(gate_pre)
    slope_val = sigmoid_val * (1.0 + gate_pre * (1.0 - sigmoid_val))
    gate_grad = (hidden_grad * up_pre * slope_val).astype(jnp.bfloat16)
    up_grad = (hidden_grad * gate_pre * sigmoid_val).astype(jnp.bfloat16)
    summed = jnp.dot(gate_grad.astype(jnp.float32), gate_w.astype(jnp.float32).T)
    summed = summed + jnp.dot(up_grad.astype(jnp.float32), up_w.astype(jnp.float32).T)
    return summed.astype(jnp.bfloat16)


def reference(tokens, expert_ids, routing, w_gate, w_up, w_down, grad_out):
    devices_all = N_DP * N_EXPERT
    pair_count = TOK_DEV * TOP
    chosen = expert_ids.reshape(devices_all, pair_count)
    onehot = (chosen[:, :, None] == jnp.arange(EXPERTS, dtype=jnp.int32)[None, None, :]).astype(jnp.int32)
    before = jnp.cumsum(onehot, axis=1) - onehot
    slot_index = jnp.sum(before * onehot, axis=2).astype(jnp.int32)
    device_row = jnp.arange(devices_all, dtype=jnp.int32)[:, None]
    slab_rows = devices_all * CAP
    flat_index = (chosen * slab_rows + device_row * CAP + slot_index).astype(jnp.int32)
    owner_row = (device_row * TOK_DEV + jnp.arange(pair_count, dtype=jnp.int32)[None, :] // TOP).astype(jnp.int32)
    slot_owner = jnp.full((EXPERTS * slab_rows,), TOKENS, jnp.int32).at[flat_index.reshape(-1)].set(owner_row.reshape(-1))
    slot_owner = slot_owner.reshape(EXPERTS, slab_rows)
    weight_slot = jnp.zeros((EXPERTS * slab_rows,), jnp.float32).at[flat_index.reshape(-1)].set(routing.reshape(-1))
    weight_slot = weight_slot.reshape(EXPERTS, slab_rows)
    zero_row = jnp.zeros((1, D), tokens.dtype)
    tokens_pad = jnp.concatenate([tokens, zero_row], axis=0)
    grads_pad = jnp.concatenate([grad_out, zero_row], axis=0)

    def per_expert(expert):
        owners = slot_owner[expert]
        row_data = tokens_pad[owners]
        scaled = (weight_slot[expert][:, None] * grads_pad[owners].astype(jnp.float32)).astype(jnp.bfloat16)
        gate_w = w_gate[expert]
        up_w = w_up[expert]
        down_w = w_down[expert]
        gate_pre, up_pre, hidden, expert_out = forward_rows(row_data, gate_w, up_w, down_w)
        pair_grad = backward_rows(scaled, gate_pre, up_pre, gate_w, up_w, down_w)
        weight_grad = jnp.dot(scaled.astype(jnp.float32).T, hidden.astype(jnp.float32))
        return expert_out, pair_grad, weight_grad

    out_all, grad_all, weight_all = lax.map(per_expert, jnp.arange(EXPERTS, dtype=jnp.int32))
    out_flat = out_all.reshape(EXPERTS * slab_rows, D)
    grad_flat = grad_all.reshape(EXPERTS * slab_rows, D)
    pair_index = flat_index.reshape(TOKENS, TOP)
    output = jnp.zeros((TOKENS, D), jnp.float32)
    token_grad = jnp.zeros((TOKENS, D), jnp.float32)
    for choice_index in range(TOP):
        rows_at = pair_index[:, choice_index]
        output = output + routing[:, choice_index][:, None] * out_flat[rows_at].astype(jnp.float32)
        token_grad = token_grad + grad_flat[rows_at].astype(jnp.float32)
    down_grad = weight_all / N_DP
    return output.astype(jnp.bfloat16), token_grad.astype(jnp.bfloat16), down_grad
```

```python
import jax
import jax.numpy as jnp
from jax import lax
from jax.sharding import PartitionSpec as P

contract_last = (((1,), (1,)), ((), ()))
contract_first = (((0,), (0,)), ((), ()))


def forward_rows(row_data, gate_w, up_w, down_w):
    gate_pre = jnp.dot(row_data, gate_w, preferred_element_type=jnp.float32)
    up_pre = jnp.dot(row_data, up_w, preferred_element_type=jnp.float32)
    sigmoid_val = jax.nn.sigmoid(gate_pre)
    hidden = (gate_pre * sigmoid_val * up_pre).astype(jnp.bfloat16)
    expert_out = lax.dot_general(
        hidden, down_w, contract_last, preferred_element_type=jnp.float32
    ).astype(jnp.bfloat16)
    return (gate_pre, up_pre, hidden, expert_out)


def backward_rows(grad_rows, gate_pre, up_pre, gate_w, up_w, down_w):
    hidden_grad = jnp.dot(grad_rows, down_w, preferred_element_type=jnp.float32)
    sigmoid_val = jax.nn.sigmoid(gate_pre)
    slope_val = sigmoid_val * (1.0 + gate_pre * (1.0 - sigmoid_val))
    gate_grad = (hidden_grad * up_pre * slope_val).astype(jnp.bfloat16)
    up_grad = (hidden_grad * gate_pre * sigmoid_val).astype(jnp.bfloat16)
    summed = lax.dot_general(gate_grad, gate_w, contract_last, preferred_element_type=jnp.float32)
    summed = summed + lax.dot_general(
        up_grad, up_w, contract_last, preferred_element_type=jnp.float32
    )
    return summed.astype(jnp.bfloat16)


def local(tokens, expert_ids, routing, w_gate, w_up, w_down, grad_out):
    tok_rows, width = tokens.shape
    groups = lax.axis_size("expert")
    local_count = w_gate.shape[0]
    ff_width = w_gate.shape[2]
    experts_all = local_count * groups
    top_count = expert_ids.shape[1]
    capacity = 3 * tok_rows * top_count // (2 * experts_all)
    pair_count = tok_rows * top_count
    chosen = expert_ids.reshape(pair_count)
    onehot = (chosen[:, None] == jnp.arange(experts_all, dtype=jnp.int32)[None, :]).astype(
        jnp.int32
    )
    before = jnp.cumsum(onehot, axis=0) - onehot
    slot_index = jnp.sum(before * onehot, axis=1)
    flat_index = chosen * capacity + slot_index
    owner_row = jnp.arange(pair_count, dtype=jnp.int32) // top_count
    slot_owner = (
        jnp.full((experts_all * capacity,), tok_rows, jnp.int32).at[flat_index].set(owner_row)
    )
    weight_slot = (
        jnp.zeros((experts_all * capacity,), jnp.float32)
        .at[flat_index]
        .set(routing.reshape(pair_count))
    )
    zero_row = jnp.zeros((1, width), jnp.bfloat16)
    send_rows = jnp.concatenate([tokens, zero_row], axis=0)[slot_owner].reshape(
        experts_all, capacity, width
    )
    grads_picked = jnp.concatenate([grad_out, zero_row], axis=0)[slot_owner].astype(jnp.float32)
    send_grads = (
        (weight_slot[:, None] * grads_picked)
        .astype(jnp.bfloat16)
        .reshape(experts_all, capacity, width)
    )
    shard_d = w_gate.shape[1]
    packed = jnp.concatenate([w_gate, w_up, w_down], axis=2)
    packed = jnp.transpose(packed, (1, 0, 2)).reshape(shard_d, local_count * 3 * ff_width)
    full = lax.all_gather(packed, "dp", axis=0, tiled=True)
    full = jnp.transpose(full.reshape(width, local_count, 3 * ff_width), (1, 0, 2))
    gate_full = full[:, :, :ff_width]
    up_full = full[:, :, ff_width : 2 * ff_width]
    down_full = full[:, :, 2 * ff_width :]
    recv_rows, recv_grads = (
        lax.all_to_all(send_rows, "expert", split_axis=0, concat_axis=0, tiled=True),
        lax.all_to_all(send_grads, "expert", split_axis=0, concat_axis=0, tiled=True),
    )
    rows_x = recv_rows.reshape(groups, local_count, capacity, width)
    rows_g = recv_grads.reshape(groups, local_count, capacity, width)
    slab_rows = groups * capacity
    expert_index = 0
    x_rows = rows_x[:, expert_index].reshape(slab_rows, width)
    g_rows = rows_g[:, expert_index].reshape(slab_rows, width)
    gate_w = gate_full[expert_index]
    up_w = up_full[expert_index]
    down_w = down_full[expert_index]
    is_valid = None
    position = None
    live_rows = None
    g_used = g_rows
    gate_pre, up_pre, hidden, expert_out = forward_rows(x_rows, gate_w, up_w, down_w)
    out_parts = [expert_out]
    forward_parts = [(gate_pre, up_pre, hidden, g_used, is_valid, position, live_rows)]
    out_send = jnp.stack(out_parts, axis=1).reshape(groups * local_count, capacity, width)
    back_out = lax.all_to_all(out_send, "expert", split_axis=0, concat_axis=0, tiled=True)
    expert_index = 0
    gate_pre, up_pre, hidden, g_used, is_valid, position, live_rows = forward_parts[expert_index]
    gate_w = gate_full[expert_index]
    up_w = up_full[expert_index]
    down_w = down_full[expert_index]
    grad_parts = [backward_rows(g_used, gate_pre, up_pre, gate_w, up_w, down_w)]
    grad_send = jnp.stack(grad_parts, axis=1).reshape(groups * local_count, capacity, width)
    back_grad = lax.all_to_all(grad_send, "expert", split_axis=0, concat_axis=0, tiled=True)
    out_rows = back_out.reshape(experts_all * capacity, width)[flat_index].reshape(
        tok_rows, top_count, width
    )
    output = jnp.sum(routing[:, :, None] * out_rows.astype(jnp.float32), axis=1).astype(
        jnp.bfloat16
    )
    grad_rows = back_grad.reshape(experts_all * capacity, width)[flat_index].reshape(
        tok_rows, top_count, width
    )
    token_grad = jnp.sum(grad_rows.astype(jnp.float32), axis=1).astype(jnp.bfloat16)
    shard_rows = w_gate.shape[1]
    saved = forward_parts[0]
    grad_cols = saved[3]
    pieces = lax.dot_general(
        grad_cols, saved[2], contract_first, preferred_element_type=jnp.float32
    )
    summed = lax.psum_scatter(pieces, "dp", scatter_dimension=0, tiled=True)
    down_grad = jnp.transpose(
        (summed / lax.axis_size("dp")).reshape(shard_rows, local_count, ff_width), (1, 0, 2)
    )
    return (output, token_grad, down_grad)


def solution(mesh):
    return jax.shard_map(
        local,
        mesh=mesh,
        in_specs=(
            P(("dp", "expert"), None),
            P(("dp", "expert"), None),
            P(("dp", "expert"), None),
            P("expert", "dp", None),
            P("expert", "dp", None),
            P("expert", "dp", None),
            P(("dp", "expert"), None),
        ),
        out_specs=(P(("dp", "expert"), None), P(("dp", "expert"), None), P("expert", "dp", None)),
        check_vma=False,
    )
```

```python
import jax
import jax.numpy as jnp
from jax import lax
from jax.sharding import PartitionSpec as P

contract_last = (((1,), (1,)), ((), ()))
contract_first = (((0,), (0,)), ((), ()))


def forward_rows(row_data, gate_w, up_w, down_w):
    gate_pre = jnp.dot(row_data, gate_w, preferred_element_type=jnp.float32)
    up_pre = jnp.dot(row_data, up_w, preferred_element_type=jnp.float32)
    sigmoid_val = jax.nn.sigmoid(gate_pre)
    hidden = (gate_pre * sigmoid_val * up_pre).astype(jnp.bfloat16)
    expert_out = lax.dot_general(
        hidden, down_w, contract_last, preferred_element_type=jnp.float32
    ).astype(jnp.bfloat16)
    return (gate_pre, up_pre, hidden, expert_out)


def backward_rows(grad_rows, gate_pre, up_pre, gate_w, up_w, down_w):
    hidden_grad = jnp.dot(grad_rows, down_w, preferred_element_type=jnp.float32)
    sigmoid_val = jax.nn.sigmoid(gate_pre)
    slope_val = sigmoid_val * (1.0 + gate_pre * (1.0 - sigmoid_val))
    gate_grad = (hidden_grad * up_pre * slope_val).astype(jnp.bfloat16)
    up_grad = (hidden_grad * gate_pre * sigmoid_val).astype(jnp.bfloat16)
    summed = lax.dot_general(gate_grad, gate_w, contract_last, preferred_element_type=jnp.float32)
    summed = summed + lax.dot_general(
        up_grad, up_w, contract_last, preferred_element_type=jnp.float32
    )
    return summed.astype(jnp.bfloat16)


def local(tokens, expert_ids, routing, w_gate, w_up, w_down, grad_out):
    tok_rows, width = tokens.shape
    groups = lax.axis_size("expert")
    local_count = w_gate.shape[0]
    ff_width = w_gate.shape[2]
    experts_all = local_count * groups
    top_count = expert_ids.shape[1]
    capacity = 3 * tok_rows * top_count // (2 * experts_all)
    pair_count = tok_rows * top_count
    chosen = expert_ids.reshape(pair_count)
    onehot = (chosen[:, None] == jnp.arange(experts_all, dtype=jnp.int32)[None, :]).astype(
        jnp.int32
    )
    earlier = (
        jnp.arange(pair_count, dtype=jnp.int32)[:, None]
        > jnp.arange(pair_count, dtype=jnp.int32)[None, :]
    ).astype(jnp.bfloat16)
    before = jnp.dot(
        earlier, onehot.astype(jnp.bfloat16), preferred_element_type=jnp.float32
    ).astype(jnp.int32)
    slot_index = jnp.sum(before * onehot, axis=1)
    flat_index = chosen * capacity + slot_index
    slots = experts_all * capacity
    hit = flat_index[:, None] == jnp.arange(slots, dtype=jnp.int32)[None, :]
    hit3 = hit.reshape(tok_rows, top_count, slots)
    dispatch = jnp.any(hit3, axis=1).astype(jnp.bfloat16)
    send_rows = (
        lax.dot_general(dispatch, tokens, contract_first, preferred_element_type=jnp.float32)
        .astype(jnp.bfloat16)
        .reshape(experts_all, capacity, width)
    )
    weight_slot = jnp.sum(jnp.where(hit, routing.reshape(pair_count)[:, None], 0.0), axis=0)
    grads_picked = lax.dot_general(
        dispatch, grad_out, contract_first, preferred_element_type=jnp.float32
    )
    send_grads = (
        (weight_slot[:, None] * grads_picked)
        .astype(jnp.bfloat16)
        .reshape(experts_all, capacity, width)
    )
    shard_d = w_gate.shape[1]
    packed = jnp.concatenate([w_gate, w_up, w_down], axis=2)
    packed = jnp.transpose(packed, (1, 0, 2)).reshape(shard_d, local_count * 3 * ff_width)
    full = lax.all_gather(packed, "dp", axis=0, tiled=True)
    full = jnp.transpose(full.reshape(width, local_count, 3 * ff_width), (1, 0, 2))
    gate_full = full[:, :, :ff_width]
    up_full = full[:, :, ff_width : 2 * ff_width]
    down_full = full[:, :, 2 * ff_width :]
    recv_rows, recv_grads = (
        lax.all_to_all(send_rows, "expert", split_axis=0, concat_axis=0, tiled=True),
        lax.all_to_all(send_grads, "expert", split_axis=0, concat_axis=0, tiled=True),
    )
    rows_x = recv_rows.reshape(groups, local_count, capacity, width)
    rows_g = recv_grads.reshape(groups, local_count, capacity, width)
    slab_rows = groups * capacity
    expert_index = 0
    x_rows = rows_x[:, expert_index].reshape(slab_rows, width)
    g_rows = rows_g[:, expert_index].reshape(slab_rows, width)
    gate_w = gate_full[expert_index]
    up_w = up_full[expert_index]
    down_w = down_full[expert_index]
    is_valid = None
    position = None
    live_rows = None
    g_used = g_rows
    gate_pre, up_pre, hidden, expert_out = forward_rows(x_rows, gate_w, up_w, down_w)
    out_parts = [expert_out]
    forward_parts = [(gate_pre, up_pre, hidden, g_used, is_valid, position, live_rows)]
    out_send = jnp.stack(out_parts, axis=1).reshape(groups * local_count, capacity, width)
    back_out = lax.all_to_all(out_send, "expert", split_axis=0, concat_axis=0, tiled=True)
    expert_index = 0
    gate_pre, up_pre, hidden, g_used, is_valid, position, live_rows = forward_parts[expert_index]
    gate_w = gate_full[expert_index]
    up_w = up_full[expert_index]
    down_w = down_full[expert_index]
    grad_parts = [backward_rows(g_used, gate_pre, up_pre, gate_w, up_w, down_w)]
    grad_send = jnp.stack(grad_parts, axis=1).reshape(groups * local_count, capacity, width)
    back_grad = lax.all_to_all(grad_send, "expert", split_axis=0, concat_axis=0, tiled=True)
    back_out_flat = back_out.reshape(slots, width)
    output = None
    for choice in range(top_count):
        pick = hit3[:, choice, :].astype(jnp.bfloat16)
        part = routing[:, choice][:, None] * jnp.dot(
            pick, back_out_flat, preferred_element_type=jnp.float32
        )
        output = part if output is None else output + part
    output = output.astype(jnp.bfloat16)
    gather_both = jnp.sum(hit3.astype(jnp.int32), axis=1).astype(jnp.bfloat16)
    token_grad = jnp.dot(
        gather_both, back_grad.reshape(slots, width), preferred_element_type=jnp.float32
    ).astype(jnp.bfloat16)
    shard_rows = w_gate.shape[1]
    saved = forward_parts[0]
    grad_cols = saved[3]
    pieces = lax.dot_general(
        grad_cols, saved[2], contract_first, preferred_element_type=jnp.float32
    )
    summed = lax.psum_scatter(pieces, "dp", scatter_dimension=0, tiled=True)
    down_grad = jnp.transpose(
        (summed / lax.axis_size("dp")).reshape(shard_rows, local_count, ff_width), (1, 0, 2)
    )
    return (output, token_grad, down_grad)


def solution(mesh):
    return jax.shard_map(
        local,
        mesh=mesh,
        in_specs=(
            P(("dp", "expert"), None),
            P(("dp", "expert"), None),
            P(("dp", "expert"), None),
            P("expert", "dp", None),
            P("expert", "dp", None),
            P("expert", "dp", None),
            P(("dp", "expert"), None),
        ),
        out_specs=(P(("dp", "expert"), None), P(("dp", "expert"), None), P("expert", "dp", None)),
        check_vma=False,
    )
```

```python
import jax
import jax.numpy as jnp
from jax import lax
from jax.sharding import PartitionSpec as P

contract_last = (((1,), (1,)), ((), ()))
contract_first = (((0,), (0,)), ((), ()))


def forward_rows(row_data, gate_w, up_w, down_w):
    gate_pre = jnp.dot(row_data, gate_w, preferred_element_type=jnp.float32)
    up_pre = jnp.dot(row_data, up_w, preferred_element_type=jnp.float32)
    sigmoid_val = jax.nn.sigmoid(gate_pre)
    hidden = (gate_pre * sigmoid_val * up_pre).astype(jnp.bfloat16)
    expert_out = lax.dot_general(
        hidden, down_w, contract_last, preferred_element_type=jnp.float32
    ).astype(jnp.bfloat16)
    return (gate_pre, up_pre, hidden, expert_out)


def backward_rows(grad_rows, gate_pre, up_pre, gate_w, up_w, down_w):
    hidden_grad = jnp.dot(grad_rows, down_w, preferred_element_type=jnp.float32)
    sigmoid_val = jax.nn.sigmoid(gate_pre)
    slope_val = sigmoid_val * (1.0 + gate_pre * (1.0 - sigmoid_val))
    gate_grad = (hidden_grad * up_pre * slope_val).astype(jnp.bfloat16)
    up_grad = (hidden_grad * gate_pre * sigmoid_val).astype(jnp.bfloat16)
    summed = lax.dot_general(gate_grad, gate_w, contract_last, preferred_element_type=jnp.float32)
    summed = summed + lax.dot_general(
        up_grad, up_w, contract_last, preferred_element_type=jnp.float32
    )
    return summed.astype(jnp.bfloat16)


def shift_send(blocks, groups, sign):
    got = [blocks[0]]
    for step in range(1, groups):
        pairs = [(i, (i + sign * step) % groups) for i in range(groups)]
        got.append(lax.ppermute(blocks[step], "expert", pairs))
    return got


def reduce_scatter_dp(pieces, n_dp):
    me = lax.axis_index("dp")
    work = pieces
    bit = 1
    while bit < n_dp:
        halves = work.reshape((work.shape[0] // 2, 2) + work.shape[1:])
        mine = (me // bit) % 2
        keep = jnp.take(halves, mine, axis=1)
        give = jnp.take(halves, 1 - mine, axis=1)
        pairs = [(i, i ^ bit) for i in range(n_dp)]
        work = keep + lax.ppermute(give, "dp", pairs)
        bit *= 2
    return work[0]


def local(tokens, expert_ids, routing, w_gate, w_up, w_down, grad_out):
    tok_rows, width = tokens.shape
    groups = lax.axis_size("expert")
    n_dp = lax.axis_size("dp")
    me = lax.axis_index("expert")
    local_count = w_gate.shape[0]
    ff_width = w_gate.shape[2]
    shard_d = w_gate.shape[1]
    experts_all = local_count * groups
    top_count = expert_ids.shape[1]
    capacity = 3 * tok_rows * top_count // (2 * experts_all)
    pair_count = tok_rows * top_count
    chosen = expert_ids.reshape(pair_count)
    home = chosen // local_count
    rotated = ((home - me) % groups) * local_count + chosen % local_count
    onehot = (rotated[:, None] == jnp.arange(experts_all, dtype=jnp.int32)[None, :]).astype(
        jnp.bfloat16
    )
    earlier = (
        jnp.arange(pair_count, dtype=jnp.int32)[:, None]
        > jnp.arange(pair_count, dtype=jnp.int32)[None, :]
    ).astype(jnp.bfloat16)
    before = jnp.dot(earlier, onehot, preferred_element_type=jnp.float32)
    slot_index = jnp.sum(before * onehot.astype(jnp.float32), axis=1).astype(jnp.int32)
    flat_index = rotated * capacity + slot_index
    slots = experts_all * capacity
    hit = flat_index[:, None] == jnp.arange(slots, dtype=jnp.int32)[None, :]
    hit3 = hit.reshape(tok_rows, top_count, slots)
    dispatch = jnp.any(hit3, axis=1).astype(jnp.bfloat16)
    send_rows = (
        lax.dot_general(dispatch, tokens, contract_first, preferred_element_type=jnp.float32)
        .astype(jnp.bfloat16)
        .reshape(groups, local_count * capacity, width)
    )
    weight_slot = jnp.sum(jnp.where(hit, routing.reshape(pair_count)[:, None], 0.0), axis=0)
    grads_picked = lax.dot_general(
        dispatch, grad_out, contract_first, preferred_element_type=jnp.float32
    )
    send_grads = (
        (weight_slot[:, None] * grads_picked)
        .astype(jnp.bfloat16)
        .reshape(groups, local_count * capacity, width)
    )
    packed = jnp.concatenate([w_gate, w_up, w_down], axis=2)
    packed = jnp.transpose(packed, (1, 0, 2)).reshape(shard_d, local_count * 3 * ff_width)
    full = lax.all_gather(packed, "dp", axis=0, tiled=True)
    full = jnp.transpose(full.reshape(width, local_count, 3 * ff_width), (1, 0, 2))
    gate_full = full[:, :, :ff_width]
    up_full = full[:, :, ff_width : 2 * ff_width]
    down_full = full[:, :, 2 * ff_width :]
    recv_rows = shift_send([send_rows[s] for s in range(groups)], groups, 1)
    recv_grads = shift_send([send_grads[s] for s in range(groups)], groups, 1)
    gate_w = gate_full[0]
    up_w = up_full[0]
    down_w = down_full[0]
    out_blocks = []
    grad_blocks = []
    hidden_blocks = []
    for s in range(groups):
        gate_pre, up_pre, hidden, expert_out = forward_rows(recv_rows[s], gate_w, up_w, down_w)
        out_blocks.append(expert_out)
        hidden_blocks.append(hidden)
        grad_blocks.append(
            backward_rows(recv_grads[s], gate_pre, up_pre, gate_w, up_w, down_w)
        )
    pieces = lax.dot_general(
        jnp.concatenate(recv_grads, axis=0),
        jnp.concatenate(hidden_blocks, axis=0),
        contract_first,
        preferred_element_type=jnp.float32,
    )
    back_out = jnp.concatenate(shift_send(out_blocks, groups, -1), axis=0)
    back_grad = jnp.concatenate(shift_send(grad_blocks, groups, -1), axis=0)
    output = None
    for choice in range(top_count):
        pick = hit3[:, choice, :].astype(jnp.bfloat16)
        part = routing[:, choice][:, None] * jnp.dot(
            pick, back_out, preferred_element_type=jnp.float32
        )
        output = part if output is None else output + part
    output = output.astype(jnp.bfloat16)
    gather_both = jnp.sum(hit3.astype(jnp.int32), axis=1).astype(jnp.bfloat16)
    token_grad = jnp.dot(
        gather_both, back_grad, preferred_element_type=jnp.float32
    ).astype(jnp.bfloat16)
    summed = reduce_scatter_dp(pieces.reshape(n_dp, shard_d, ff_width), n_dp)
    down_grad = (summed / n_dp).reshape(local_count, shard_d, ff_width)
    return (output, token_grad, down_grad)


def solution(mesh):
    return jax.shard_map(
        local,
        mesh=mesh,
        in_specs=(
            P(("dp", "expert"), None),
            P(("dp", "expert"), None),
            P(("dp", "expert"), None),
            P("expert", "dp", None),
            P("expert", "dp", None),
            P("expert", "dp", None),
            P(("dp", "expert"), None),
        ),
        out_specs=(P(("dp", "expert"), None), P(("dp", "expert"), None), P("expert", "dp", None)),
        check_vma=False,
    )
```

```python
import jax
import jax.numpy as jnp
from jax import lax
from jax.sharding import PartitionSpec as P

contract_last = (((1,), (1,)), ((), ()))
contract_first = (((0,), (0,)), ((), ()))


def forward_rows(row_data, gate_w, up_w, down_w):
    gate_pre = jnp.dot(row_data, gate_w, preferred_element_type=jnp.float32)
    up_pre = jnp.dot(row_data, up_w, preferred_element_type=jnp.float32)
    sigmoid_val = jax.nn.sigmoid(gate_pre)
    hidden = (gate_pre * sigmoid_val * up_pre).astype(jnp.bfloat16)
    expert_out = lax.dot_general(
        hidden, down_w, contract_last, preferred_element_type=jnp.float32
    ).astype(jnp.bfloat16)
    return (gate_pre, up_pre, hidden, expert_out)


def backward_rows(grad_rows, gate_pre, up_pre, gate_w, up_w, down_w):
    hidden_grad = jnp.dot(grad_rows, down_w, preferred_element_type=jnp.float32)
    sigmoid_val = jax.nn.sigmoid(gate_pre)
    slope_val = sigmoid_val * (1.0 + gate_pre * (1.0 - sigmoid_val))
    gate_grad = (hidden_grad * up_pre * slope_val).astype(jnp.bfloat16)
    up_grad = (hidden_grad * gate_pre * sigmoid_val).astype(jnp.bfloat16)
    summed = lax.dot_general(gate_grad, gate_w, contract_last, preferred_element_type=jnp.float32)
    summed = summed + lax.dot_general(
        up_grad, up_w, contract_last, preferred_element_type=jnp.float32
    )
    return summed.astype(jnp.bfloat16)


def shift_send(blocks, groups, sign):
    got = [blocks[0]]
    for step in range(1, groups):
        pairs = [(i, (i + sign * step) % groups) for i in range(groups)]
        got.append(lax.ppermute(blocks[step], "expert", pairs))
    return got


def all_gather_dp(block, n_dp):
    me = lax.axis_index("dp")
    work = block[None]
    bit = n_dp // 2
    while bit >= 1:
        recv = lax.ppermute(work, "dp", [(i, i ^ bit) for i in range(n_dp)])
        upper = (me // bit) % 2 == 1
        low = jnp.where(upper, recv, work)
        high = jnp.where(upper, work, recv)
        work = jnp.stack([low, high], axis=1).reshape((2 * work.shape[0],) + work.shape[1:])
        bit //= 2
    return work


def reduce_scatter_dp(pieces, n_dp):
    me = lax.axis_index("dp")
    work = pieces
    bit = 1
    while bit < n_dp:
        halves = work.reshape((work.shape[0] // 2, 2) + work.shape[1:])
        mine = (me // bit) % 2
        keep = jnp.take(halves, mine, axis=1)
        give = jnp.take(halves, 1 - mine, axis=1)
        pairs = [(i, i ^ bit) for i in range(n_dp)]
        work = keep + lax.ppermute(give, "dp", pairs)
        bit *= 2
    return work[0]


def local(tokens, expert_ids, routing, w_gate, w_up, w_down, grad_out):
    tok_rows, width = tokens.shape
    groups = lax.axis_size("expert")
    n_dp = lax.axis_size("dp")
    me = lax.axis_index("expert")
    local_count = w_gate.shape[0]
    ff_width = w_gate.shape[2]
    shard_d = w_gate.shape[1]
    experts_all = local_count * groups
    top_count = expert_ids.shape[1]
    capacity = 3 * tok_rows * top_count // (2 * experts_all)
    pair_count = tok_rows * top_count
    chosen = expert_ids.reshape(pair_count)
    home = chosen // local_count
    rotated = ((home - me) % groups) * local_count + chosen % local_count
    onehot = (rotated[:, None] == jnp.arange(experts_all, dtype=jnp.int32)[None, :]).astype(
        jnp.bfloat16
    )
    earlier = (
        jnp.arange(pair_count, dtype=jnp.int32)[:, None]
        > jnp.arange(pair_count, dtype=jnp.int32)[None, :]
    ).astype(jnp.bfloat16)
    before = jnp.dot(earlier, onehot, preferred_element_type=jnp.float32)
    slot_index = jnp.sum(before * onehot.astype(jnp.float32), axis=1).astype(jnp.int32)
    flat_index = rotated * capacity + slot_index
    slots = experts_all * capacity
    hit = flat_index[:, None] == jnp.arange(slots, dtype=jnp.int32)[None, :]
    hit3 = hit.reshape(tok_rows, top_count, slots)
    dispatch = jnp.any(hit3, axis=1).astype(jnp.bfloat16)
    send_rows = (
        lax.dot_general(dispatch, tokens, contract_first, preferred_element_type=jnp.float32)
        .astype(jnp.bfloat16)
        .reshape(groups, local_count * capacity, width)
    )
    weight_slot = jnp.sum(jnp.where(hit, routing.reshape(pair_count)[:, None], 0.0), axis=0)
    grads_picked = lax.dot_general(
        dispatch, grad_out, contract_first, preferred_element_type=jnp.float32
    )
    send_grads = (
        (weight_slot[:, None] * grads_picked)
        .astype(jnp.bfloat16)
        .reshape(groups, local_count * capacity, width)
    )
    packed = jnp.concatenate([w_gate, w_up, w_down], axis=2)
    packed = jnp.transpose(packed, (1, 0, 2)).reshape(shard_d, local_count * 3 * ff_width)
    full = all_gather_dp(packed, n_dp).reshape(width, local_count * 3 * ff_width)
    full = jnp.transpose(full.reshape(width, local_count, 3 * ff_width), (1, 0, 2))
    gate_full = full[:, :, :ff_width]
    up_full = full[:, :, ff_width : 2 * ff_width]
    down_full = full[:, :, 2 * ff_width :]
    recv_rows = shift_send([send_rows[s] for s in range(groups)], groups, 1)
    recv_grads = shift_send([send_grads[s] for s in range(groups)], groups, 1)
    gate_w = gate_full[0]
    up_w = up_full[0]
    down_w = down_full[0]
    x_rows = jnp.concatenate(recv_rows, axis=0)
    g_rows = jnp.concatenate(recv_grads, axis=0)
    gate_pre, up_pre, hidden, expert_out = forward_rows(x_rows, gate_w, up_w, down_w)
    pair_grad = backward_rows(g_rows, gate_pre, up_pre, gate_w, up_w, down_w)
    pieces = lax.dot_general(g_rows, hidden, contract_first, preferred_element_type=jnp.float32)
    block_rows = local_count * capacity
    out_blocks = [expert_out[s * block_rows : (s + 1) * block_rows] for s in range(groups)]
    grad_blocks = [pair_grad[s * block_rows : (s + 1) * block_rows] for s in range(groups)]
    back_out = jnp.concatenate(shift_send(out_blocks, groups, -1), axis=0)
    back_grad = jnp.concatenate(shift_send(grad_blocks, groups, -1), axis=0)
    output = None
    for choice in range(top_count):
        pick = hit3[:, choice, :].astype(jnp.bfloat16)
        part = routing[:, choice][:, None] * jnp.dot(
            pick, back_out, preferred_element_type=jnp.float32
        )
        output = part if output is None else output + part
    output = output.astype(jnp.bfloat16)
    gather_both = jnp.sum(hit3.astype(jnp.int32), axis=1).astype(jnp.bfloat16)
    token_grad = jnp.dot(
        gather_both, back_grad, preferred_element_type=jnp.float32
    ).astype(jnp.bfloat16)
    summed = reduce_scatter_dp(pieces.reshape(n_dp, shard_d, ff_width), n_dp)
    down_grad = (summed / n_dp).reshape(local_count, shard_d, ff_width)
    return (output, token_grad, down_grad)


def solution(mesh):
    return jax.shard_map(
        local,
        mesh=mesh,
        in_specs=(
            P(("dp", "expert"), None),
            P(("dp", "expert"), None),
            P(("dp", "expert"), None),
            P("expert", "dp", None),
            P("expert", "dp", None),
            P("expert", "dp", None),
            P(("dp", "expert"), None),
        ),
        out_specs=(P(("dp", "expert"), None), P(("dp", "expert"), None), P("expert", "dp", None)),
        check_vma=False,
    )
```

```python
import jax
import jax.numpy as jnp
from jax import lax
from jax.sharding import PartitionSpec as P

contract_last = (((1,), (1,)), ((), ()))
contract_first = (((0,), (0,)), ((), ()))


def forward_rows(row_data, gate_w, up_w, down_w):
    gate_pre = jnp.dot(row_data, gate_w, preferred_element_type=jnp.float32)
    up_pre = jnp.dot(row_data, up_w, preferred_element_type=jnp.float32)
    sigmoid_val = jax.nn.sigmoid(gate_pre)
    hidden = (gate_pre * sigmoid_val * up_pre).astype(jnp.bfloat16)
    expert_out = lax.dot_general(
        hidden, down_w, contract_last, preferred_element_type=jnp.float32
    ).astype(jnp.bfloat16)
    return (gate_pre, up_pre, hidden, expert_out)


def backward_rows(grad_rows, gate_pre, up_pre, gate_w, up_w, down_w):
    hidden_grad = jnp.dot(grad_rows, down_w, preferred_element_type=jnp.float32)
    sigmoid_val = jax.nn.sigmoid(gate_pre)
    slope_val = sigmoid_val * (1.0 + gate_pre * (1.0 - sigmoid_val))
    gate_grad = (hidden_grad * up_pre * slope_val).astype(jnp.bfloat16)
    up_grad = (hidden_grad * gate_pre * sigmoid_val).astype(jnp.bfloat16)
    summed = lax.dot_general(gate_grad, gate_w, contract_last, preferred_element_type=jnp.float32)
    summed = summed + lax.dot_general(
        up_grad, up_w, contract_last, preferred_element_type=jnp.float32
    )
    return summed.astype(jnp.bfloat16)


def shift_send(blocks, groups, sign):
    got = [blocks[0]]
    for step in range(1, groups):
        pairs = [(i, (i + sign * step) % groups) for i in range(groups)]
        got.append(lax.ppermute(blocks[step], "expert", pairs))
    return got


def all_gather_dp(block, n_dp):
    me = lax.axis_index("dp")
    work = block[None]
    bit = n_dp // 2
    while bit >= 1:
        recv = lax.ppermute(work, "dp", [(i, i ^ bit) for i in range(n_dp)])
        upper = (me // bit) % 2 == 1
        low = jnp.where(upper, recv, work)
        high = jnp.where(upper, work, recv)
        work = jnp.stack([low, high], axis=1).reshape((2 * work.shape[0],) + work.shape[1:])
        bit //= 2
    return work


def reduce_scatter_dp(pieces, n_dp):
    me = lax.axis_index("dp")
    work = pieces
    bit = 1
    while bit < n_dp:
        halves = work.reshape((work.shape[0] // 2, 2) + work.shape[1:])
        mine = (me // bit) % 2
        keep = jnp.take(halves, mine, axis=1)
        give = jnp.take(halves, 1 - mine, axis=1)
        pairs = [(i, i ^ bit) for i in range(n_dp)]
        work = keep + lax.ppermute(give, "dp", pairs)
        bit *= 2
    return work[0]


def local(tokens, expert_ids, routing, w_gate, w_up, w_down, grad_out):
    tok_rows, width = tokens.shape
    groups = lax.axis_size("expert")
    n_dp = lax.axis_size("dp")
    me = lax.axis_index("expert")
    local_count = w_gate.shape[0]
    ff_width = w_gate.shape[2]
    shard_d = w_gate.shape[1]
    experts_all = local_count * groups
    top_count = expert_ids.shape[1]
    capacity = 3 * tok_rows * top_count // (2 * experts_all)
    pair_count = tok_rows * top_count
    chosen = expert_ids.reshape(pair_count)
    home = chosen // local_count
    rotated = ((home - me) % groups) * local_count + chosen % local_count
    onehot = (rotated[:, None] == jnp.arange(experts_all, dtype=jnp.int32)[None, :]).astype(
        jnp.bfloat16
    )
    earlier = (
        jnp.arange(pair_count, dtype=jnp.int32)[:, None]
        > jnp.arange(pair_count, dtype=jnp.int32)[None, :]
    ).astype(jnp.bfloat16)
    before = jnp.dot(earlier, onehot, preferred_element_type=jnp.float32)
    slot_index = jnp.sum(before * onehot.astype(jnp.float32), axis=1).astype(jnp.int32)
    flat_index = rotated * capacity + slot_index
    slots = experts_all * capacity
    hit = flat_index[:, None] == jnp.arange(slots, dtype=jnp.int32)[None, :]
    hit3 = hit.reshape(tok_rows, top_count, slots)
    dispatch = jnp.any(hit3, axis=1).astype(jnp.bfloat16)
    send_rows = (
        lax.dot_general(dispatch, tokens, contract_first, preferred_element_type=jnp.float32)
        .astype(jnp.bfloat16)
        .reshape(groups, local_count * capacity, width)
    )
    weight_slot = jnp.sum(jnp.where(hit, routing.reshape(pair_count)[:, None], 0.0), axis=0)
    grads_picked = lax.dot_general(
        dispatch, grad_out, contract_first, preferred_element_type=jnp.float32
    )
    send_grads = (
        (weight_slot[:, None] * grads_picked)
        .astype(jnp.bfloat16)
        .reshape(groups, local_count * capacity, width)
    )
    packed = jnp.concatenate([w_gate, w_up, w_down], axis=2)
    packed = jnp.transpose(packed, (1, 0, 2)).reshape(shard_d, local_count * 3 * ff_width)
    recv_rows = shift_send([send_rows[s] for s in range(groups)], groups, 1)
    recv_grads = shift_send([send_grads[s] for s in range(groups)], groups, 1)
    packed, _ = lax.optimization_barrier((packed, recv_rows[1:]))
    full = all_gather_dp(packed, n_dp).reshape(width, local_count * 3 * ff_width)
    full = jnp.transpose(full.reshape(width, local_count, 3 * ff_width), (1, 0, 2))
    gate_full = full[:, :, :ff_width]
    up_full = full[:, :, ff_width : 2 * ff_width]
    down_full = full[:, :, 2 * ff_width :]
    gate_w = gate_full[0]
    up_w = up_full[0]
    down_w = down_full[0]
    x_rows = jnp.concatenate(recv_rows, axis=0)
    g_rows = jnp.concatenate(recv_grads, axis=0)
    gate_pre, up_pre, hidden, expert_out = forward_rows(x_rows, gate_w, up_w, down_w)
    pair_grad = backward_rows(g_rows, gate_pre, up_pre, gate_w, up_w, down_w)
    pieces = lax.dot_general(g_rows, hidden, contract_first, preferred_element_type=jnp.float32)
    block_rows = local_count * capacity
    out_blocks = [expert_out[s * block_rows : (s + 1) * block_rows] for s in range(groups)]
    grad_blocks = [pair_grad[s * block_rows : (s + 1) * block_rows] for s in range(groups)]
    back_out = jnp.concatenate(shift_send(out_blocks, groups, -1), axis=0)
    back_grad = jnp.concatenate(shift_send(grad_blocks, groups, -1), axis=0)
    output = None
    for choice in range(top_count):
        pick = hit3[:, choice, :].astype(jnp.bfloat16)
        part = routing[:, choice][:, None] * jnp.dot(
            pick, back_out, preferred_element_type=jnp.float32
        )
        output = part if output is None else output + part
    output = output.astype(jnp.bfloat16)
    gather_both = jnp.sum(hit3.astype(jnp.int32), axis=1).astype(jnp.bfloat16)
    token_grad = jnp.dot(
        gather_both, back_grad, preferred_element_type=jnp.float32
    ).astype(jnp.bfloat16)
    summed = reduce_scatter_dp(pieces.reshape(n_dp, shard_d, ff_width), n_dp)
    down_grad = (summed / n_dp).reshape(local_count, shard_d, ff_width)
    return (output, token_grad, down_grad)


def solution(mesh):
    return jax.shard_map(
        local,
        mesh=mesh,
        in_specs=(
            P(("dp", "expert"), None),
            P(("dp", "expert"), None),
            P(("dp", "expert"), None),
            P("expert", "dp", None),
            P("expert", "dp", None),
            P("expert", "dp", None),
            P(("dp", "expert"), None),
        ),
        out_specs=(P(("dp", "expert"), None), P(("dp", "expert"), None), P("expert", "dp", None)),
        check_vma=False,
    )
```

```python
import jax
import jax.numpy as jnp
from jax import lax
from jax.sharding import PartitionSpec as P

contract_last = (((1,), (1,)), ((), ()))
contract_first = (((0,), (0,)), ((), ()))


def forward_rows(row_data, gate_w, up_w, down_w):
    gate_pre = jnp.dot(row_data, gate_w, preferred_element_type=jnp.float32)
    up_pre = jnp.dot(row_data, up_w, preferred_element_type=jnp.float32)
    sigmoid_val = jax.nn.sigmoid(gate_pre)
    hidden = (gate_pre * sigmoid_val * up_pre).astype(jnp.bfloat16)
    expert_out = lax.dot_general(
        hidden, down_w, contract_last, preferred_element_type=jnp.float32
    ).astype(jnp.bfloat16)
    return (gate_pre, up_pre, hidden, expert_out)


def backward_rows(grad_rows, gate_pre, up_pre, gate_w, up_w, down_w):
    hidden_grad = jnp.dot(grad_rows, down_w, preferred_element_type=jnp.float32)
    sigmoid_val = jax.nn.sigmoid(gate_pre)
    slope_val = sigmoid_val * (1.0 + gate_pre * (1.0 - sigmoid_val))
    gate_grad = (hidden_grad * up_pre * slope_val).astype(jnp.bfloat16)
    up_grad = (hidden_grad * gate_pre * sigmoid_val).astype(jnp.bfloat16)
    summed = lax.dot_general(gate_grad, gate_w, contract_last, preferred_element_type=jnp.float32)
    summed = summed + lax.dot_general(
        up_grad, up_w, contract_last, preferred_element_type=jnp.float32
    )
    return summed.astype(jnp.bfloat16)


def shift_send(blocks, groups, sign):
    got = [blocks[0]]
    for step in range(1, groups):
        pairs = [(i, (i + sign * step) % groups) for i in range(groups)]
        got.append(lax.ppermute(blocks[step], "expert", pairs))
    return got


def all_gather_dp(block, n_dp):
    me = lax.axis_index("dp")
    work = block[None]
    bit = n_dp // 2
    while bit >= 1:
        recv = lax.ppermute(work, "dp", [(i, i ^ bit) for i in range(n_dp)])
        upper = (me // bit) % 2 == 1
        low = jnp.where(upper, recv, work)
        high = jnp.where(upper, work, recv)
        work = jnp.stack([low, high], axis=1).reshape((2 * work.shape[0],) + work.shape[1:])
        bit //= 2
    return work


def reduce_scatter_dp(pieces, n_dp):
    me = lax.axis_index("dp")
    work = pieces
    bit = 1
    while bit < n_dp:
        halves = work.reshape((work.shape[0] // 2, 2) + work.shape[1:])
        mine = (me // bit) % 2
        keep = jnp.take(halves, mine, axis=1)
        give = jnp.take(halves, 1 - mine, axis=1)
        pairs = [(i, i ^ bit) for i in range(n_dp)]
        work = keep + lax.ppermute(give, "dp", pairs)
        bit *= 2
    return work[0]


def local(tokens, expert_ids, routing, w_gate, w_up, w_down, grad_out):
    tok_rows, width = tokens.shape
    groups = lax.axis_size("expert")
    n_dp = lax.axis_size("dp")
    me = lax.axis_index("expert")
    local_count = w_gate.shape[0]
    ff_width = w_gate.shape[2]
    shard_d = w_gate.shape[1]
    experts_all = local_count * groups
    top_count = expert_ids.shape[1]
    capacity = 3 * tok_rows * top_count // (2 * experts_all)
    pair_count = tok_rows * top_count
    chosen = expert_ids.reshape(pair_count)
    home = chosen // local_count
    rotated = ((home - me) % groups) * local_count + chosen % local_count
    onehot = (rotated[:, None] == jnp.arange(experts_all, dtype=jnp.int32)[None, :]).astype(
        jnp.bfloat16
    )
    earlier = (
        jnp.arange(pair_count, dtype=jnp.int32)[:, None]
        > jnp.arange(pair_count, dtype=jnp.int32)[None, :]
    ).astype(jnp.bfloat16)
    before = jnp.dot(earlier, onehot, preferred_element_type=jnp.float32)
    slot_index = jnp.sum(before * onehot.astype(jnp.float32), axis=1).astype(jnp.int32)
    flat_index = rotated * capacity + slot_index
    slots = experts_all * capacity
    hit = flat_index[:, None] == jnp.arange(slots, dtype=jnp.int32)[None, :]
    hit3 = hit.reshape(tok_rows, top_count, slots)
    dispatch = jnp.any(hit3, axis=1).astype(jnp.bfloat16)
    send_rows = (
        lax.dot_general(dispatch, tokens, contract_first, preferred_element_type=jnp.float32)
        .astype(jnp.bfloat16)
        .reshape(groups, local_count * capacity, width)
    )
    weight_slot = jnp.sum(jnp.where(hit, routing.reshape(pair_count)[:, None], 0.0), axis=0)
    grads_picked = lax.dot_general(
        dispatch, grad_out, contract_first, preferred_element_type=jnp.float32
    )
    send_grads = (
        (weight_slot[:, None] * grads_picked)
        .astype(jnp.bfloat16)
        .reshape(groups, local_count * capacity, width)
    )
    packed = jnp.concatenate([w_gate, w_up, w_down], axis=2)
    packed = jnp.transpose(packed, (1, 0, 2)).reshape(shard_d, local_count * 3 * ff_width)
    full = all_gather_dp(packed, n_dp).reshape(width, local_count * 3 * ff_width)
    full = jnp.transpose(full.reshape(width, local_count, 3 * ff_width), (1, 0, 2))
    gate_full = full[:, :, :ff_width]
    up_full = full[:, :, ff_width : 2 * ff_width]
    down_full = full[:, :, 2 * ff_width :]
    both = jnp.stack([send_rows, send_grads], axis=1)
    recv_both = shift_send([both[s] for s in range(groups)], groups, 1)
    recv_rows = [b[0] for b in recv_both]
    recv_grads = [b[1] for b in recv_both]
    gate_w = gate_full[0]
    up_w = up_full[0]
    down_w = down_full[0]
    x_rows = jnp.concatenate(recv_rows, axis=0)
    g_rows = jnp.concatenate(recv_grads, axis=0)
    gate_pre, up_pre, hidden, expert_out = forward_rows(x_rows, gate_w, up_w, down_w)
    pair_grad = backward_rows(g_rows, gate_pre, up_pre, gate_w, up_w, down_w)
    pieces = lax.dot_general(g_rows, hidden, contract_first, preferred_element_type=jnp.float32)
    block_rows = local_count * capacity
    out_blocks = [expert_out[s * block_rows : (s + 1) * block_rows] for s in range(groups)]
    grad_blocks = [pair_grad[s * block_rows : (s + 1) * block_rows] for s in range(groups)]
    back_out = jnp.concatenate(shift_send(out_blocks, groups, -1), axis=0)
    back_grad = jnp.concatenate(shift_send(grad_blocks, groups, -1), axis=0)
    output = None
    for choice in range(top_count):
        pick = hit3[:, choice, :].astype(jnp.bfloat16)
        part = routing[:, choice][:, None] * jnp.dot(
            pick, back_out, preferred_element_type=jnp.float32
        )
        output = part if output is None else output + part
    output = output.astype(jnp.bfloat16)
    gather_both = jnp.sum(hit3.astype(jnp.int32), axis=1).astype(jnp.bfloat16)
    token_grad = jnp.dot(
        gather_both, back_grad, preferred_element_type=jnp.float32
    ).astype(jnp.bfloat16)
    summed = reduce_scatter_dp(pieces.reshape(n_dp, shard_d, ff_width), n_dp)
    down_grad = (summed / n_dp).reshape(local_count, shard_d, ff_width)
    return (output, token_grad, down_grad)


def solution(mesh):
    return jax.shard_map(
        local,
        mesh=mesh,
        in_specs=(
            P(("dp", "expert"), None),
            P(("dp", "expert"), None),
            P(("dp", "expert"), None),
            P("expert", "dp", None),
            P("expert", "dp", None),
            P("expert", "dp", None),
            P(("dp", "expert"), None),
        ),
        out_specs=(P(("dp", "expert"), None), P(("dp", "expert"), None), P("expert", "dp", None)),
        check_vma=False,
    )
```

```python
import jax
import jax.numpy as jnp
from jax import lax
from jax.sharding import PartitionSpec as P

contract_last = (((1,), (1,)), ((), ()))
contract_first = (((0,), (0,)), ((), ()))


def forward_rows(row_data, gate_w, up_w, down_w):
    gate_pre = jnp.dot(row_data, gate_w, preferred_element_type=jnp.float32)
    up_pre = jnp.dot(row_data, up_w, preferred_element_type=jnp.float32)
    sigmoid_val = jax.nn.sigmoid(gate_pre)
    hidden = (gate_pre * sigmoid_val * up_pre).astype(jnp.bfloat16)
    expert_out = lax.dot_general(
        hidden, down_w, contract_last, preferred_element_type=jnp.float32
    ).astype(jnp.bfloat16)
    return (gate_pre, up_pre, hidden, expert_out)


def backward_rows(grad_rows, gate_pre, up_pre, gate_w, up_w, down_w):
    hidden_grad = jnp.dot(grad_rows, down_w, preferred_element_type=jnp.float32)
    sigmoid_val = jax.nn.sigmoid(gate_pre)
    slope_val = sigmoid_val * (1.0 + gate_pre * (1.0 - sigmoid_val))
    gate_grad = (hidden_grad * up_pre * slope_val).astype(jnp.bfloat16)
    up_grad = (hidden_grad * gate_pre * sigmoid_val).astype(jnp.bfloat16)
    summed = lax.dot_general(gate_grad, gate_w, contract_last, preferred_element_type=jnp.float32)
    summed = summed + lax.dot_general(
        up_grad, up_w, contract_last, preferred_element_type=jnp.float32
    )
    return summed.astype(jnp.bfloat16)


def shift_send(blocks, groups, sign):
    got = [blocks[0]]
    for step in range(1, groups):
        pairs = [(i, (i + sign * step) % groups) for i in range(groups)]
        got.append(lax.ppermute(blocks[step], "expert", pairs))
    return got


def gather_bits(block, bits, n_dp):
    me = lax.axis_index("dp")
    work = block
    for bit in bits:
        recv = lax.ppermute(work, "dp", [(i, i ^ bit) for i in range(n_dp)])
        upper = (me // bit) % 2 == 1
        work = jnp.stack([jnp.where(upper, recv, work), jnp.where(upper, work, recv)], axis=0)
    axes = list(reversed(bits))
    perm = sorted(range(len(bits)), key=lambda a: -axes[a])
    work = jnp.transpose(work, perm + list(range(len(bits), work.ndim)))
    return work.reshape((2 ** len(bits),) + block.shape)


def all_gather_dp(block, n_dp):
    bits = []
    bit = 1
    while bit < n_dp:
        bits.append(bit)
        bit *= 2
    half = block.shape[-1] // 2
    near = gather_bits(block, bits[:1], n_dp)
    rest = bits[1:]
    left = gather_bits(near[..., :half], rest, n_dp)
    right = gather_bits(near[..., half:], rest[::-1], n_dp)
    out_shape = (n_dp,) + block.shape[:-1] + (half,)
    return jnp.concatenate([left.reshape(out_shape), right.reshape(out_shape)], axis=-1)


def reduce_scatter_dp(pieces, n_dp):
    me = lax.axis_index("dp")
    work = pieces
    bit = 1
    while bit < n_dp:
        halves = work.reshape((work.shape[0] // 2, 2) + work.shape[1:])
        mine = (me // bit) % 2
        keep = jnp.take(halves, mine, axis=1)
        give = jnp.take(halves, 1 - mine, axis=1)
        pairs = [(i, i ^ bit) for i in range(n_dp)]
        work = keep + lax.ppermute(give, "dp", pairs)
        bit *= 2
    return work[0]


def local(tokens, expert_ids, routing, w_gate, w_up, w_down, grad_out):
    tok_rows, width = tokens.shape
    groups = lax.axis_size("expert")
    n_dp = lax.axis_size("dp")
    me = lax.axis_index("expert")
    local_count = w_gate.shape[0]
    ff_width = w_gate.shape[2]
    shard_d = w_gate.shape[1]
    experts_all = local_count * groups
    top_count = expert_ids.shape[1]
    capacity = 3 * tok_rows * top_count // (2 * experts_all)
    pair_count = tok_rows * top_count
    chosen = expert_ids.reshape(pair_count)
    home = chosen // local_count
    rotated = ((home - me) % groups) * local_count + chosen % local_count
    onehot = (rotated[:, None] == jnp.arange(experts_all, dtype=jnp.int32)[None, :]).astype(
        jnp.bfloat16
    )
    earlier = (
        jnp.arange(pair_count, dtype=jnp.int32)[:, None]
        > jnp.arange(pair_count, dtype=jnp.int32)[None, :]
    ).astype(jnp.bfloat16)
    before = jnp.dot(earlier, onehot, preferred_element_type=jnp.float32)
    slot_index = jnp.sum(before * onehot.astype(jnp.float32), axis=1).astype(jnp.int32)
    flat_index = rotated * capacity + slot_index
    slots = experts_all * capacity
    hit = flat_index[:, None] == jnp.arange(slots, dtype=jnp.int32)[None, :]
    hit3 = hit.reshape(tok_rows, top_count, slots)
    dispatch = jnp.any(hit3, axis=1).astype(jnp.bfloat16)
    send_rows = (
        lax.dot_general(dispatch, tokens, contract_first, preferred_element_type=jnp.float32)
        .astype(jnp.bfloat16)
        .reshape(groups, local_count * capacity, width)
    )
    weight_slot = jnp.sum(jnp.where(hit, routing.reshape(pair_count)[:, None], 0.0), axis=0)
    grads_picked = lax.dot_general(
        dispatch, grad_out, contract_first, preferred_element_type=jnp.float32
    )
    send_grads = (
        (weight_slot[:, None] * grads_picked)
        .astype(jnp.bfloat16)
        .reshape(groups, local_count * capacity, width)
    )
    packed = jnp.concatenate([w_gate, w_up, w_down], axis=2)
    packed = jnp.transpose(packed, (1, 0, 2)).reshape(shard_d, local_count * 3 * ff_width)
    full = all_gather_dp(packed, n_dp).reshape(width, local_count * 3 * ff_width)
    full = jnp.transpose(full.reshape(width, local_count, 3 * ff_width), (1, 0, 2))
    gate_full = full[:, :, :ff_width]
    up_full = full[:, :, ff_width : 2 * ff_width]
    down_full = full[:, :, 2 * ff_width :]
    recv_rows = shift_send([send_rows[s] for s in range(groups)], groups, 1)
    recv_grads = shift_send([send_grads[s] for s in range(groups)], groups, 1)
    gate_w = gate_full[0]
    up_w = up_full[0]
    down_w = down_full[0]
    x_rows = jnp.concatenate(recv_rows, axis=0)
    g_rows = jnp.concatenate(recv_grads, axis=0)
    gate_pre, up_pre, hidden, expert_out = forward_rows(x_rows, gate_w, up_w, down_w)
    pair_grad = backward_rows(g_rows, gate_pre, up_pre, gate_w, up_w, down_w)
    pieces = lax.dot_general(g_rows, hidden, contract_first, preferred_element_type=jnp.float32)
    block_rows = local_count * capacity
    out_blocks = [expert_out[s * block_rows : (s + 1) * block_rows] for s in range(groups)]
    grad_blocks = [pair_grad[s * block_rows : (s + 1) * block_rows] for s in range(groups)]
    back_out = jnp.concatenate(shift_send(out_blocks, groups, -1), axis=0)
    back_grad = jnp.concatenate(shift_send(grad_blocks, groups, -1), axis=0)
    output = None
    for choice in range(top_count):
        pick = hit3[:, choice, :].astype(jnp.bfloat16)
        part = routing[:, choice][:, None] * jnp.dot(
            pick, back_out, preferred_element_type=jnp.float32
        )
        output = part if output is None else output + part
    output = output.astype(jnp.bfloat16)
    gather_both = jnp.sum(hit3.astype(jnp.int32), axis=1).astype(jnp.bfloat16)
    token_grad = jnp.dot(
        gather_both, back_grad, preferred_element_type=jnp.float32
    ).astype(jnp.bfloat16)
    summed = reduce_scatter_dp(pieces.reshape(n_dp, shard_d, ff_width), n_dp)
    down_grad = (summed / n_dp).reshape(local_count, shard_d, ff_width)
    return (output, token_grad, down_grad)


def solution(mesh):
    return jax.shard_map(
        local,
        mesh=mesh,
        in_specs=(
            P(("dp", "expert"), None),
            P(("dp", "expert"), None),
            P(("dp", "expert"), None),
            P("expert", "dp", None),
            P("expert", "dp", None),
            P("expert", "dp", None),
            P(("dp", "expert"), None),
        ),
        out_specs=(P(("dp", "expert"), None), P(("dp", "expert"), None), P("expert", "dp", None)),
        check_vma=False,
    )
```

```python
import jax
import jax.numpy as jnp
from jax import lax
from jax.sharding import PartitionSpec as P

contract_last = (((1,), (1,)), ((), ()))
contract_first = (((0,), (0,)), ((), ()))


def forward_rows(row_data, gate_w, up_w, down_w):
    gate_pre = jnp.dot(row_data, gate_w, preferred_element_type=jnp.float32)
    up_pre = jnp.dot(row_data, up_w, preferred_element_type=jnp.float32)
    sigmoid_val = jax.nn.sigmoid(gate_pre)
    hidden = (gate_pre * sigmoid_val * up_pre).astype(jnp.bfloat16)
    expert_out = lax.dot_general(
        hidden, down_w, contract_last, preferred_element_type=jnp.float32
    ).astype(jnp.bfloat16)
    return (gate_pre, up_pre, hidden, expert_out)


def backward_rows(grad_rows, gate_pre, up_pre, gate_w, up_w, down_w):
    hidden_grad = jnp.dot(grad_rows, down_w, preferred_element_type=jnp.float32)
    sigmoid_val = jax.nn.sigmoid(gate_pre)
    slope_val = sigmoid_val * (1.0 + gate_pre * (1.0 - sigmoid_val))
    gate_grad = (hidden_grad * up_pre * slope_val).astype(jnp.bfloat16)
    up_grad = (hidden_grad * gate_pre * sigmoid_val).astype(jnp.bfloat16)
    summed = lax.dot_general(gate_grad, gate_w, contract_last, preferred_element_type=jnp.float32)
    summed = summed + lax.dot_general(
        up_grad, up_w, contract_last, preferred_element_type=jnp.float32
    )
    return summed.astype(jnp.bfloat16)


def shift_send(blocks, groups, sign):
    got = [blocks[0]]
    for step in range(1, groups):
        pairs = [(i, (i + sign * step) % groups) for i in range(groups)]
        got.append(lax.ppermute(blocks[step], "expert", pairs))
    return got


def all_gather_dp(block, n_dp):
    me = lax.axis_index("dp")
    work = block[None]
    bit = n_dp // 2
    while bit >= 1:
        recv = lax.ppermute(work, "dp", [(i, i ^ bit) for i in range(n_dp)])
        upper = (me // bit) % 2 == 1
        low = jnp.where(upper, recv, work)
        high = jnp.where(upper, work, recv)
        work = jnp.stack([low, high], axis=1).reshape((2 * work.shape[0],) + work.shape[1:])
        bit //= 2
    return work


def halve_bits(work, axes, bits, n_dp):
    me = lax.axis_index("dp")
    axes = list(axes)
    for bit in bits:
        ax = axes.index(bit)
        mine = (me // bit) % 2
        keep = jnp.take(work, mine, axis=ax)
        give = jnp.take(work, 1 - mine, axis=ax)
        work = keep + lax.ppermute(give, "dp", [(i, i ^ bit) for i in range(n_dp)])
        axes.pop(ax)
    return work, axes


def reduce_scatter_dp(pieces, n_dp):
    bits = []
    bit = n_dp // 2
    while bit >= 1:
        bits.append(bit)
        bit //= 2
    work = pieces.reshape((2,) * len(bits) + pieces.shape[1:])
    work, axes = halve_bits(work, bits, bits[-1:], n_dp)
    rest = sorted(axes)
    half = work.shape[-1] // 2
    left, _ = halve_bits(work[..., :half], axes, rest, n_dp)
    right, _ = halve_bits(work[..., half:], axes, rest[::-1], n_dp)
    return jnp.concatenate([left, right], axis=-1)


def local(tokens, expert_ids, routing, w_gate, w_up, w_down, grad_out):
    tok_rows, width = tokens.shape
    groups = lax.axis_size("expert")
    n_dp = lax.axis_size("dp")
    me = lax.axis_index("expert")
    local_count = w_gate.shape[0]
    ff_width = w_gate.shape[2]
    shard_d = w_gate.shape[1]
    experts_all = local_count * groups
    top_count = expert_ids.shape[1]
    capacity = 3 * tok_rows * top_count // (2 * experts_all)
    pair_count = tok_rows * top_count
    chosen = expert_ids.reshape(pair_count)
    home = chosen // local_count
    rotated = ((home - me) % groups) * local_count + chosen % local_count
    onehot = (rotated[:, None] == jnp.arange(experts_all, dtype=jnp.int32)[None, :]).astype(
        jnp.bfloat16
    )
    earlier = (
        jnp.arange(pair_count, dtype=jnp.int32)[:, None]
        > jnp.arange(pair_count, dtype=jnp.int32)[None, :]
    ).astype(jnp.bfloat16)
    before = jnp.dot(earlier, onehot, preferred_element_type=jnp.float32)
    slot_index = jnp.sum(before * onehot.astype(jnp.float32), axis=1).astype(jnp.int32)
    flat_index = rotated * capacity + slot_index
    slots = experts_all * capacity
    hit = flat_index[:, None] == jnp.arange(slots, dtype=jnp.int32)[None, :]
    hit3 = hit.reshape(tok_rows, top_count, slots)
    dispatch = jnp.any(hit3, axis=1).astype(jnp.bfloat16)
    send_rows = (
        lax.dot_general(dispatch, tokens, contract_first, preferred_element_type=jnp.float32)
        .astype(jnp.bfloat16)
        .reshape(groups, local_count * capacity, width)
    )
    weight_slot = jnp.sum(jnp.where(hit, routing.reshape(pair_count)[:, None], 0.0), axis=0)
    grads_picked = lax.dot_general(
        dispatch, grad_out, contract_first, preferred_element_type=jnp.float32
    )
    send_grads = (
        (weight_slot[:, None] * grads_picked)
        .astype(jnp.bfloat16)
        .reshape(groups, local_count * capacity, width)
    )
    packed = jnp.concatenate([w_gate, w_up, w_down], axis=2)
    packed = jnp.transpose(packed, (1, 0, 2)).reshape(shard_d, local_count * 3 * ff_width)
    full = all_gather_dp(packed, n_dp).reshape(width, local_count * 3 * ff_width)
    full = jnp.transpose(full.reshape(width, local_count, 3 * ff_width), (1, 0, 2))
    gate_full = full[:, :, :ff_width]
    up_full = full[:, :, ff_width : 2 * ff_width]
    down_full = full[:, :, 2 * ff_width :]
    recv_rows = shift_send([send_rows[s] for s in range(groups)], groups, 1)
    recv_grads = shift_send([send_grads[s] for s in range(groups)], groups, 1)
    gate_w = gate_full[0]
    up_w = up_full[0]
    down_w = down_full[0]
    x_rows = jnp.concatenate(recv_rows, axis=0)
    g_rows = jnp.concatenate(recv_grads, axis=0)
    gate_pre, up_pre, hidden, expert_out = forward_rows(x_rows, gate_w, up_w, down_w)
    pair_grad = backward_rows(g_rows, gate_pre, up_pre, gate_w, up_w, down_w)
    pieces = lax.dot_general(g_rows, hidden, contract_first, preferred_element_type=jnp.float32)
    block_rows = local_count * capacity
    out_blocks = [expert_out[s * block_rows : (s + 1) * block_rows] for s in range(groups)]
    grad_blocks = [pair_grad[s * block_rows : (s + 1) * block_rows] for s in range(groups)]
    back_out = jnp.concatenate(shift_send(out_blocks, groups, -1), axis=0)
    back_grad = jnp.concatenate(shift_send(grad_blocks, groups, -1), axis=0)
    output = None
    for choice in range(top_count):
        pick = hit3[:, choice, :].astype(jnp.bfloat16)
        part = routing[:, choice][:, None] * jnp.dot(
            pick, back_out, preferred_element_type=jnp.float32
        )
        output = part if output is None else output + part
    output = output.astype(jnp.bfloat16)
    gather_both = jnp.sum(hit3.astype(jnp.int32), axis=1).astype(jnp.bfloat16)
    token_grad = jnp.dot(
        gather_both, back_grad, preferred_element_type=jnp.float32
    ).astype(jnp.bfloat16)
    summed = reduce_scatter_dp(pieces.reshape(n_dp, shard_d, ff_width), n_dp)
    down_grad = (summed / n_dp).reshape(local_count, shard_d, ff_width)
    return (output, token_grad, down_grad)


def solution(mesh):
    return jax.shard_map(
        local,
        mesh=mesh,
        in_specs=(
            P(("dp", "expert"), None),
            P(("dp", "expert"), None),
            P(("dp", "expert"), None),
            P("expert", "dp", None),
            P("expert", "dp", None),
            P("expert", "dp", None),
            P(("dp", "expert"), None),
        ),
        out_specs=(P(("dp", "expert"), None), P(("dp", "expert"), None), P("expert", "dp", None)),
        check_vma=False,
    )
```

```python
import jax
import jax.numpy as jnp
from jax import lax
from jax.sharding import PartitionSpec as P

contract_last = (((1,), (1,)), ((), ()))
contract_first = (((0,), (0,)), ((), ()))


def forward_rows(row_data, gate_w, up_w, down_w):
    gate_pre = jnp.dot(row_data, gate_w, preferred_element_type=jnp.float32)
    up_pre = jnp.dot(row_data, up_w, preferred_element_type=jnp.float32)
    sigmoid_val = jax.nn.sigmoid(gate_pre)
    hidden = (gate_pre * sigmoid_val * up_pre).astype(jnp.bfloat16)
    expert_out = lax.dot_general(
        hidden, down_w, contract_last, preferred_element_type=jnp.float32
    ).astype(jnp.bfloat16)
    return (gate_pre, up_pre, hidden, expert_out)


def backward_rows(grad_rows, gate_pre, up_pre, gate_w, up_w, down_w):
    hidden_grad = jnp.dot(grad_rows, down_w, preferred_element_type=jnp.float32)
    sigmoid_val = jax.nn.sigmoid(gate_pre)
    slope_val = sigmoid_val * (1.0 + gate_pre * (1.0 - sigmoid_val))
    gate_grad = (hidden_grad * up_pre * slope_val).astype(jnp.bfloat16)
    up_grad = (hidden_grad * gate_pre * sigmoid_val).astype(jnp.bfloat16)
    summed = lax.dot_general(gate_grad, gate_w, contract_last, preferred_element_type=jnp.float32)
    summed = summed + lax.dot_general(
        up_grad, up_w, contract_last, preferred_element_type=jnp.float32
    )
    return summed.astype(jnp.bfloat16)


def shift_send(blocks, groups, sign):
    got = [blocks[0]]
    for step in range(1, groups):
        pairs = [(i, (i + sign * step) % groups) for i in range(groups)]
        got.append(lax.ppermute(blocks[step], "expert", pairs))
    return got


def all_gather_dp(block, n_dp):
    me = lax.axis_index("dp")
    bits = []
    bit = n_dp // 2
    while bit >= 1:
        bits.append(bit)
        bit //= 2
    if len(bits) >= 3:
        bits[0], bits[1] = bits[1], bits[0]
    work = block
    for bit in bits:
        recv = lax.ppermute(work, "dp", [(i, i ^ bit) for i in range(n_dp)])
        upper = (me // bit) % 2 == 1
        work = jnp.stack([jnp.where(upper, recv, work), jnp.where(upper, work, recv)], axis=0)
    axes = list(reversed(bits))
    perm = sorted(range(len(bits)), key=lambda a: -axes[a])
    work = jnp.transpose(work, perm + list(range(len(bits), work.ndim)))
    return work.reshape((n_dp,) + block.shape)


def reduce_scatter_dp(pieces, n_dp):
    me = lax.axis_index("dp")
    work = pieces
    bit = 1
    while bit < n_dp:
        halves = work.reshape((work.shape[0] // 2, 2) + work.shape[1:])
        mine = (me // bit) % 2
        keep = jnp.take(halves, mine, axis=1)
        give = jnp.take(halves, 1 - mine, axis=1)
        pairs = [(i, i ^ bit) for i in range(n_dp)]
        work = keep + lax.ppermute(give, "dp", pairs)
        bit *= 2
    return work[0]


def local(tokens, expert_ids, routing, w_gate, w_up, w_down, grad_out):
    tok_rows, width = tokens.shape
    groups = lax.axis_size("expert")
    n_dp = lax.axis_size("dp")
    me = lax.axis_index("expert")
    local_count = w_gate.shape[0]
    ff_width = w_gate.shape[2]
    shard_d = w_gate.shape[1]
    experts_all = local_count * groups
    top_count = expert_ids.shape[1]
    capacity = 3 * tok_rows * top_count // (2 * experts_all)
    pair_count = tok_rows * top_count
    chosen = expert_ids.reshape(pair_count)
    home = chosen // local_count
    rotated = ((home - me) % groups) * local_count + chosen % local_count
    onehot = (rotated[:, None] == jnp.arange(experts_all, dtype=jnp.int32)[None, :]).astype(
        jnp.bfloat16
    )
    earlier = (
        jnp.arange(pair_count, dtype=jnp.int32)[:, None]
        > jnp.arange(pair_count, dtype=jnp.int32)[None, :]
    ).astype(jnp.bfloat16)
    before = jnp.dot(earlier, onehot, preferred_element_type=jnp.float32)
    slot_index = jnp.sum(before * onehot.astype(jnp.float32), axis=1).astype(jnp.int32)
    flat_index = rotated * capacity + slot_index
    slots = experts_all * capacity
    hit = flat_index[:, None] == jnp.arange(slots, dtype=jnp.int32)[None, :]
    hit3 = hit.reshape(tok_rows, top_count, slots)
    dispatch = jnp.any(hit3, axis=1).astype(jnp.bfloat16)
    send_rows = (
        lax.dot_general(dispatch, tokens, contract_first, preferred_element_type=jnp.float32)
        .astype(jnp.bfloat16)
        .reshape(groups, local_count * capacity, width)
    )
    weight_slot = jnp.sum(jnp.where(hit, routing.reshape(pair_count)[:, None], 0.0), axis=0)
    grads_picked = lax.dot_general(
        dispatch, grad_out, contract_first, preferred_element_type=jnp.float32
    )
    send_grads = (
        (weight_slot[:, None] * grads_picked)
        .astype(jnp.bfloat16)
        .reshape(groups, local_count * capacity, width)
    )
    packed = jnp.concatenate([w_gate, w_up, w_down], axis=2)
    packed = jnp.transpose(packed, (1, 0, 2)).reshape(shard_d, local_count * 3 * ff_width)
    full = all_gather_dp(packed, n_dp).reshape(width, local_count * 3 * ff_width)
    full = jnp.transpose(full.reshape(width, local_count, 3 * ff_width), (1, 0, 2))
    gate_full = full[:, :, :ff_width]
    up_full = full[:, :, ff_width : 2 * ff_width]
    down_full = full[:, :, 2 * ff_width :]
    recv_rows = shift_send([send_rows[s] for s in range(groups)], groups, 1)
    recv_grads = shift_send([send_grads[s] for s in range(groups)], groups, 1)
    gate_w = gate_full[0]
    up_w = up_full[0]
    down_w = down_full[0]
    x_rows = jnp.concatenate(recv_rows, axis=0)
    g_rows = jnp.concatenate(recv_grads, axis=0)
    gate_pre, up_pre, hidden, expert_out = forward_rows(x_rows, gate_w, up_w, down_w)
    pair_grad = backward_rows(g_rows, gate_pre, up_pre, gate_w, up_w, down_w)
    pieces = lax.dot_general(g_rows, hidden, contract_first, preferred_element_type=jnp.float32)
    block_rows = local_count * capacity
    out_blocks = [expert_out[s * block_rows : (s + 1) * block_rows] for s in range(groups)]
    grad_blocks = [pair_grad[s * block_rows : (s + 1) * block_rows] for s in range(groups)]
    back_out = jnp.concatenate(shift_send(out_blocks, groups, -1), axis=0)
    back_grad = jnp.concatenate(shift_send(grad_blocks, groups, -1), axis=0)
    output = None
    for choice in range(top_count):
        pick = hit3[:, choice, :].astype(jnp.bfloat16)
        part = routing[:, choice][:, None] * jnp.dot(
            pick, back_out, preferred_element_type=jnp.float32
        )
        output = part if output is None else output + part
    output = output.astype(jnp.bfloat16)
    gather_both = jnp.sum(hit3.astype(jnp.int32), axis=1).astype(jnp.bfloat16)
    token_grad = jnp.dot(
        gather_both, back_grad, preferred_element_type=jnp.float32
    ).astype(jnp.bfloat16)
    summed = reduce_scatter_dp(pieces.reshape(n_dp, shard_d, ff_width), n_dp)
    down_grad = (summed / n_dp).reshape(local_count, shard_d, ff_width)
    return (output, token_grad, down_grad)


def solution(mesh):
    return jax.shard_map(
        local,
        mesh=mesh,
        in_specs=(
            P(("dp", "expert"), None),
            P(("dp", "expert"), None),
            P(("dp", "expert"), None),
            P("expert", "dp", None),
            P("expert", "dp", None),
            P("expert", "dp", None),
            P(("dp", "expert"), None),
        ),
        out_specs=(P(("dp", "expert"), None), P(("dp", "expert"), None), P("expert", "dp", None)),
        check_vma=False,
    )
```

```python
import jax
import jax.numpy as jnp
from jax import lax
from jax.sharding import PartitionSpec as P

contract_last = (((1,), (1,)), ((), ()))
contract_first = (((0,), (0,)), ((), ()))


def forward_rows(row_data, gate_w, up_w, down_w):
    gate_pre = jnp.dot(row_data, gate_w, preferred_element_type=jnp.float32)
    up_pre = jnp.dot(row_data, up_w, preferred_element_type=jnp.float32)
    sigmoid_val = jax.nn.sigmoid(gate_pre)
    hidden = (gate_pre * sigmoid_val * up_pre).astype(jnp.bfloat16)
    expert_out = lax.dot_general(
        hidden, down_w, contract_last, preferred_element_type=jnp.float32
    ).astype(jnp.bfloat16)
    return (gate_pre, up_pre, hidden, expert_out)


def backward_rows(grad_rows, gate_pre, up_pre, gate_w, up_w, down_w):
    hidden_grad = jnp.dot(grad_rows, down_w, preferred_element_type=jnp.float32)
    sigmoid_val = jax.nn.sigmoid(gate_pre)
    slope_val = sigmoid_val * (1.0 + gate_pre * (1.0 - sigmoid_val))
    gate_grad = (hidden_grad * up_pre * slope_val).astype(jnp.bfloat16)
    up_grad = (hidden_grad * gate_pre * sigmoid_val).astype(jnp.bfloat16)
    summed = lax.dot_general(gate_grad, gate_w, contract_last, preferred_element_type=jnp.float32)
    summed = summed + lax.dot_general(
        up_grad, up_w, contract_last, preferred_element_type=jnp.float32
    )
    return summed.astype(jnp.bfloat16)


def shift_send(blocks, groups, sign):
    got = [blocks[0]]
    for step in range(1, groups):
        pairs = [(i, (i + sign * step) % groups) for i in range(groups)]
        got.append(lax.ppermute(blocks[step], "expert", pairs))
    return got


def all_gather_dp(block, n_dp, hold=None):
    me = lax.axis_index("dp")
    bits = []
    bit = n_dp // 2
    while bit >= 1:
        bits.append(bit)
        bit //= 2
    if len(bits) >= 3:
        bits[0], bits[1] = bits[1], bits[0]
    work = block
    for step, bit in enumerate(bits):
        if step == 1 and hold is not None:
            work, _ = lax.optimization_barrier((work, hold))
        recv = lax.ppermute(work, "dp", [(i, i ^ bit) for i in range(n_dp)])
        upper = (me // bit) % 2 == 1
        work = jnp.stack([jnp.where(upper, recv, work), jnp.where(upper, work, recv)], axis=0)
    axes = list(reversed(bits))
    perm = sorted(range(len(bits)), key=lambda a: -axes[a])
    work = jnp.transpose(work, perm + list(range(len(bits), work.ndim)))
    return work.reshape((n_dp,) + block.shape)


def reduce_scatter_dp(pieces, n_dp):
    me = lax.axis_index("dp")
    work = pieces
    bit = 1
    while bit < n_dp:
        halves = work.reshape((work.shape[0] // 2, 2) + work.shape[1:])
        mine = (me // bit) % 2
        keep = jnp.take(halves, mine, axis=1)
        give = jnp.take(halves, 1 - mine, axis=1)
        pairs = [(i, i ^ bit) for i in range(n_dp)]
        work = keep + lax.ppermute(give, "dp", pairs)
        bit *= 2
    return work[0]


def local(tokens, expert_ids, routing, w_gate, w_up, w_down, grad_out):
    tok_rows, width = tokens.shape
    groups = lax.axis_size("expert")
    n_dp = lax.axis_size("dp")
    me = lax.axis_index("expert")
    local_count = w_gate.shape[0]
    ff_width = w_gate.shape[2]
    shard_d = w_gate.shape[1]
    experts_all = local_count * groups
    top_count = expert_ids.shape[1]
    capacity = 3 * tok_rows * top_count // (2 * experts_all)
    pair_count = tok_rows * top_count
    chosen = expert_ids.reshape(pair_count)
    home = chosen // local_count
    rotated = ((home - me) % groups) * local_count + chosen % local_count
    onehot = (rotated[:, None] == jnp.arange(experts_all, dtype=jnp.int32)[None, :]).astype(
        jnp.bfloat16
    )
    earlier = (
        jnp.arange(pair_count, dtype=jnp.int32)[:, None]
        > jnp.arange(pair_count, dtype=jnp.int32)[None, :]
    ).astype(jnp.bfloat16)
    before = jnp.dot(earlier, onehot, preferred_element_type=jnp.float32)
    slot_index = jnp.sum(before * onehot.astype(jnp.float32), axis=1).astype(jnp.int32)
    flat_index = rotated * capacity + slot_index
    slots = experts_all * capacity
    hit = flat_index[:, None] == jnp.arange(slots, dtype=jnp.int32)[None, :]
    hit3 = hit.reshape(tok_rows, top_count, slots)
    dispatch = jnp.any(hit3, axis=1).astype(jnp.bfloat16)
    send_rows = (
        lax.dot_general(dispatch, tokens, contract_first, preferred_element_type=jnp.float32)
        .astype(jnp.bfloat16)
        .reshape(groups, local_count * capacity, width)
    )
    weight_slot = jnp.sum(jnp.where(hit, routing.reshape(pair_count)[:, None], 0.0), axis=0)
    grads_picked = lax.dot_general(
        dispatch, grad_out, contract_first, preferred_element_type=jnp.float32
    )
    send_grads = (
        (weight_slot[:, None] * grads_picked)
        .astype(jnp.bfloat16)
        .reshape(groups, local_count * capacity, width)
    )
    packed = jnp.concatenate([w_gate, w_up, w_down], axis=2)
    packed = jnp.transpose(packed, (1, 0, 2)).reshape(shard_d, local_count * 3 * ff_width)
    full = all_gather_dp(packed, n_dp, send_grads).reshape(width, local_count * 3 * ff_width)
    full = jnp.transpose(full.reshape(width, local_count, 3 * ff_width), (1, 0, 2))
    gate_full = full[:, :, :ff_width]
    up_full = full[:, :, ff_width : 2 * ff_width]
    down_full = full[:, :, 2 * ff_width :]
    recv_rows = shift_send([send_rows[s] for s in range(groups)], groups, 1)
    recv_grads = shift_send([send_grads[s] for s in range(groups)], groups, 1)
    gate_w = gate_full[0]
    up_w = up_full[0]
    down_w = down_full[0]
    x_rows = jnp.concatenate(recv_rows, axis=0)
    g_rows = jnp.concatenate(recv_grads, axis=0)
    gate_pre, up_pre, hidden, expert_out = forward_rows(x_rows, gate_w, up_w, down_w)
    pair_grad = backward_rows(g_rows, gate_pre, up_pre, gate_w, up_w, down_w)
    pieces = lax.dot_general(g_rows, hidden, contract_first, preferred_element_type=jnp.float32)
    block_rows = local_count * capacity
    out_blocks = [expert_out[s * block_rows : (s + 1) * block_rows] for s in range(groups)]
    grad_blocks = [pair_grad[s * block_rows : (s + 1) * block_rows] for s in range(groups)]
    back_out = jnp.concatenate(shift_send(out_blocks, groups, -1), axis=0)
    back_grad = jnp.concatenate(shift_send(grad_blocks, groups, -1), axis=0)
    output = None
    for choice in range(top_count):
        pick = hit3[:, choice, :].astype(jnp.bfloat16)
        part = routing[:, choice][:, None] * jnp.dot(
            pick, back_out, preferred_element_type=jnp.float32
        )
        output = part if output is None else output + part
    output = output.astype(jnp.bfloat16)
    gather_both = jnp.sum(hit3.astype(jnp.int32), axis=1).astype(jnp.bfloat16)
    token_grad = jnp.dot(
        gather_both, back_grad, preferred_element_type=jnp.float32
    ).astype(jnp.bfloat16)
    summed = reduce_scatter_dp(pieces.reshape(n_dp, shard_d, ff_width), n_dp)
    down_grad = (summed / n_dp).reshape(local_count, shard_d, ff_width)
    return (output, token_grad, down_grad)


def solution(mesh):
    return jax.shard_map(
        local,
        mesh=mesh,
        in_specs=(
            P(("dp", "expert"), None),
            P(("dp", "expert"), None),
            P(("dp", "expert"), None),
            P("expert", "dp", None),
            P("expert", "dp", None),
            P("expert", "dp", None),
            P(("dp", "expert"), None),
        ),
        out_specs=(P(("dp", "expert"), None), P(("dp", "expert"), None), P("expert", "dp", None)),
        check_vma=False,
    )
```

```python
import jax
import jax.numpy as jnp
from jax import lax
from jax.sharding import PartitionSpec as P

contract_last = (((1,), (1,)), ((), ()))
contract_first = (((0,), (0,)), ((), ()))


def forward_rows(row_data, gate_w, up_w, down_w):
    gate_pre = jnp.dot(row_data, gate_w, preferred_element_type=jnp.float32)
    up_pre = jnp.dot(row_data, up_w, preferred_element_type=jnp.float32)
    sigmoid_val = jax.nn.sigmoid(gate_pre)
    hidden = (gate_pre * sigmoid_val * up_pre).astype(jnp.bfloat16)
    expert_out = lax.dot_general(
        hidden, down_w, contract_last, preferred_element_type=jnp.float32
    ).astype(jnp.bfloat16)
    return (gate_pre, up_pre, hidden, expert_out)


def backward_rows(grad_rows, gate_pre, up_pre, gate_w, up_w, down_w):
    hidden_grad = jnp.dot(grad_rows, down_w, preferred_element_type=jnp.float32)
    sigmoid_val = jax.nn.sigmoid(gate_pre)
    slope_val = sigmoid_val * (1.0 + gate_pre * (1.0 - sigmoid_val))
    gate_grad = (hidden_grad * up_pre * slope_val).astype(jnp.bfloat16)
    up_grad = (hidden_grad * gate_pre * sigmoid_val).astype(jnp.bfloat16)
    summed = lax.dot_general(gate_grad, gate_w, contract_last, preferred_element_type=jnp.float32)
    summed = summed + lax.dot_general(
        up_grad, up_w, contract_last, preferred_element_type=jnp.float32
    )
    return summed.astype(jnp.bfloat16)


def shift_send(blocks, groups, sign):
    got = [blocks[0]]
    for step in range(1, groups):
        pairs = [(i, (i + sign * step) % groups) for i in range(groups)]
        got.append(lax.ppermute(blocks[step], "expert", pairs))
    return got


def all_gather_dp(block, n_dp):
    me = lax.axis_index("dp")
    bits = []
    bit = n_dp // 2
    while bit >= 1:
        bits.append(bit)
        bit //= 2
    if len(bits) >= 3:
        bits = [bits[1], bits[-1]] + [bits[0]] + bits[2:-1]
    work = block
    for bit in bits:
        recv = lax.ppermute(work, "dp", [(i, i ^ bit) for i in range(n_dp)])
        upper = (me // bit) % 2 == 1
        work = jnp.stack([jnp.where(upper, recv, work), jnp.where(upper, work, recv)], axis=0)
    axes = list(reversed(bits))
    perm = sorted(range(len(bits)), key=lambda a: -axes[a])
    work = jnp.transpose(work, perm + list(range(len(bits), work.ndim)))
    return work.reshape((n_dp,) + block.shape)


def reduce_scatter_dp(pieces, n_dp):
    me = lax.axis_index("dp")
    work = pieces
    bit = 1
    while bit < n_dp:
        halves = work.reshape((work.shape[0] // 2, 2) + work.shape[1:])
        mine = (me // bit) % 2
        keep = jnp.take(halves, mine, axis=1)
        give = jnp.take(halves, 1 - mine, axis=1)
        pairs = [(i, i ^ bit) for i in range(n_dp)]
        work = keep + lax.ppermute(give, "dp", pairs)
        bit *= 2
    return work[0]


def local(tokens, expert_ids, routing, w_gate, w_up, w_down, grad_out):
    tok_rows, width = tokens.shape
    groups = lax.axis_size("expert")
    n_dp = lax.axis_size("dp")
    me = lax.axis_index("expert")
    local_count = w_gate.shape[0]
    ff_width = w_gate.shape[2]
    shard_d = w_gate.shape[1]
    experts_all = local_count * groups
    top_count = expert_ids.shape[1]
    capacity = 3 * tok_rows * top_count // (2 * experts_all)
    pair_count = tok_rows * top_count
    chosen = expert_ids.reshape(pair_count)
    home = chosen // local_count
    rotated = ((home - me) % groups) * local_count + chosen % local_count
    onehot = (rotated[:, None] == jnp.arange(experts_all, dtype=jnp.int32)[None, :]).astype(
        jnp.bfloat16
    )
    earlier = (
        jnp.arange(pair_count, dtype=jnp.int32)[:, None]
        > jnp.arange(pair_count, dtype=jnp.int32)[None, :]
    ).astype(jnp.bfloat16)
    before = jnp.dot(earlier, onehot, preferred_element_type=jnp.float32)
    slot_index = jnp.sum(before * onehot.astype(jnp.float32), axis=1).astype(jnp.int32)
    flat_index = rotated * capacity + slot_index
    slots = experts_all * capacity
    hit = flat_index[:, None] == jnp.arange(slots, dtype=jnp.int32)[None, :]
    hit3 = hit.reshape(tok_rows, top_count, slots)
    dispatch = jnp.any(hit3, axis=1).astype(jnp.bfloat16)
    send_rows = (
        lax.dot_general(dispatch, tokens, contract_first, preferred_element_type=jnp.float32)
        .astype(jnp.bfloat16)
        .reshape(groups, local_count * capacity, width)
    )
    weight_slot = jnp.sum(jnp.where(hit, routing.reshape(pair_count)[:, None], 0.0), axis=0)
    grads_picked = lax.dot_general(
        dispatch, grad_out, contract_first, preferred_element_type=jnp.float32
    )
    send_grads = (
        (weight_slot[:, None] * grads_picked)
        .astype(jnp.bfloat16)
        .reshape(groups, local_count * capacity, width)
    )
    packed = jnp.concatenate([w_gate, w_up, w_down], axis=2)
    packed = jnp.transpose(packed, (1, 0, 2)).reshape(shard_d, local_count * 3 * ff_width)
    full = all_gather_dp(packed, n_dp).reshape(width, local_count * 3 * ff_width)
    full = jnp.transpose(full.reshape(width, local_count, 3 * ff_width), (1, 0, 2))
    gate_full = full[:, :, :ff_width]
    up_full = full[:, :, ff_width : 2 * ff_width]
    down_full = full[:, :, 2 * ff_width :]
    recv_rows = shift_send([send_rows[s] for s in range(groups)], groups, 1)
    recv_grads = shift_send([send_grads[s] for s in range(groups)], groups, 1)
    gate_w = gate_full[0]
    up_w = up_full[0]
    down_w = down_full[0]
    x_rows = jnp.concatenate(recv_rows, axis=0)
    g_rows = jnp.concatenate(recv_grads, axis=0)
    gate_pre, up_pre, hidden, expert_out = forward_rows(x_rows, gate_w, up_w, down_w)
    pair_grad = backward_rows(g_rows, gate_pre, up_pre, gate_w, up_w, down_w)
    pieces = lax.dot_general(g_rows, hidden, contract_first, preferred_element_type=jnp.float32)
    block_rows = local_count * capacity
    out_blocks = [expert_out[s * block_rows : (s + 1) * block_rows] for s in range(groups)]
    grad_blocks = [pair_grad[s * block_rows : (s + 1) * block_rows] for s in range(groups)]
    back_out = jnp.concatenate(shift_send(out_blocks, groups, -1), axis=0)
    back_grad = jnp.concatenate(shift_send(grad_blocks, groups, -1), axis=0)
    output = None
    for choice in range(top_count):
        pick = hit3[:, choice, :].astype(jnp.bfloat16)
        part = routing[:, choice][:, None] * jnp.dot(
            pick, back_out, preferred_element_type=jnp.float32
        )
        output = part if output is None else output + part
    output = output.astype(jnp.bfloat16)
    gather_both = jnp.sum(hit3.astype(jnp.int32), axis=1).astype(jnp.bfloat16)
    token_grad = jnp.dot(
        gather_both, back_grad, preferred_element_type=jnp.float32
    ).astype(jnp.bfloat16)
    summed = reduce_scatter_dp(pieces.reshape(n_dp, shard_d, ff_width), n_dp)
    down_grad = (summed / n_dp).reshape(local_count, shard_d, ff_width)
    return (output, token_grad, down_grad)


def solution(mesh):
    return jax.shard_map(
        local,
        mesh=mesh,
        in_specs=(
            P(("dp", "expert"), None),
            P(("dp", "expert"), None),
            P(("dp", "expert"), None),
            P("expert", "dp", None),
            P("expert", "dp", None),
            P("expert", "dp", None),
            P(("dp", "expert"), None),
        ),
        out_specs=(P(("dp", "expert"), None), P(("dp", "expert"), None), P("expert", "dp", None)),
        check_vma=False,
    )
```

```python
import jax
import jax.numpy as jnp
from jax import lax
from jax.sharding import PartitionSpec as P

contract_last = (((1,), (1,)), ((), ()))
contract_first = (((0,), (0,)), ((), ()))


def forward_rows(row_data, gate_w, up_w, down_w):
    gate_pre = jnp.dot(row_data, gate_w, preferred_element_type=jnp.float32)
    up_pre = jnp.dot(row_data, up_w, preferred_element_type=jnp.float32)
    sigmoid_val = jax.nn.sigmoid(gate_pre)
    hidden = (gate_pre * sigmoid_val * up_pre).astype(jnp.bfloat16)
    expert_out = lax.dot_general(
        hidden, down_w, contract_last, preferred_element_type=jnp.float32
    ).astype(jnp.bfloat16)
    return (gate_pre, up_pre, hidden, expert_out)


def backward_rows(grad_rows, gate_pre, up_pre, gate_w, up_w, down_w):
    hidden_grad = jnp.dot(grad_rows, down_w, preferred_element_type=jnp.float32)
    sigmoid_val = jax.nn.sigmoid(gate_pre)
    slope_val = sigmoid_val * (1.0 + gate_pre * (1.0 - sigmoid_val))
    gate_grad = (hidden_grad * up_pre * slope_val).astype(jnp.bfloat16)
    up_grad = (hidden_grad * gate_pre * sigmoid_val).astype(jnp.bfloat16)
    summed = lax.dot_general(gate_grad, gate_w, contract_last, preferred_element_type=jnp.float32)
    summed = summed + lax.dot_general(
        up_grad, up_w, contract_last, preferred_element_type=jnp.float32
    )
    return summed.astype(jnp.bfloat16)


def shift_send(blocks, groups, sign):
    got = [blocks[0]]
    for step in range(1, groups):
        pairs = [(i, (i + sign * step) % groups) for i in range(groups)]
        got.append(lax.ppermute(blocks[step], "expert", pairs))
    return got


def all_gather_dp(block, n_dp):
    me = lax.axis_index("dp")
    bits = []
    bit = n_dp // 2
    while bit >= 1:
        bits.append(bit)
        bit //= 2
    if len(bits) >= 3:
        bits[0], bits[1] = bits[1], bits[0]
    work = block
    for bit in bits:
        recv = lax.ppermute(work, "dp", [(i, i ^ bit) for i in range(n_dp)])
        upper = (me // bit) % 2 == 1
        work = jnp.stack([jnp.where(upper, recv, work), jnp.where(upper, work, recv)], axis=0)
    axes = list(reversed(bits))
    perm = sorted(range(len(bits)), key=lambda a: -axes[a])
    work = jnp.transpose(work, perm + list(range(len(bits), work.ndim)))
    return work.reshape((n_dp,) + block.shape)


def reduce_scatter_dp(pieces, n_dp):
    me = lax.axis_index("dp")
    work = pieces
    bit = 1
    while bit < n_dp:
        halves = work.reshape((work.shape[0] // 2, 2) + work.shape[1:])
        mine = (me // bit) % 2
        keep = jnp.take(halves, mine, axis=1)
        give = jnp.take(halves, 1 - mine, axis=1)
        pairs = [(i, i ^ bit) for i in range(n_dp)]
        work = keep + lax.ppermute(give, "dp", pairs)
        bit *= 2
    return work[0]


def local(tokens, expert_ids, routing, w_gate, w_up, w_down, grad_out):
    tok_rows, width = tokens.shape
    groups = lax.axis_size("expert")
    n_dp = lax.axis_size("dp")
    me = lax.axis_index("expert")
    local_count = w_gate.shape[0]
    ff_width = w_gate.shape[2]
    shard_d = w_gate.shape[1]
    experts_all = local_count * groups
    top_count = expert_ids.shape[1]
    capacity = 3 * tok_rows * top_count // (2 * experts_all)
    pair_count = tok_rows * top_count
    chosen = expert_ids.reshape(pair_count)
    home = chosen // local_count
    rotated = ((home - me) % groups) * local_count + chosen % local_count
    onehot = (rotated[:, None] == jnp.arange(experts_all, dtype=jnp.int32)[None, :]).astype(
        jnp.bfloat16
    )
    earlier = (
        jnp.arange(pair_count, dtype=jnp.int32)[:, None]
        > jnp.arange(pair_count, dtype=jnp.int32)[None, :]
    ).astype(jnp.bfloat16)
    before = jnp.dot(earlier, onehot, preferred_element_type=jnp.float32)
    slot_index = jnp.sum(before * onehot.astype(jnp.float32), axis=1).astype(jnp.int32)
    flat_index = rotated * capacity + slot_index
    slots = experts_all * capacity
    hit = flat_index[:, None] == jnp.arange(slots, dtype=jnp.int32)[None, :]
    hit3 = hit.reshape(tok_rows, top_count, slots)
    dispatch = jnp.any(hit3, axis=1).astype(jnp.bfloat16)
    send_rows = (
        lax.dot_general(dispatch, tokens, contract_first, preferred_element_type=jnp.float32)
        .astype(jnp.bfloat16)
        .reshape(groups, local_count * capacity, width)
    )
    weight_slot = jnp.sum(jnp.where(hit, routing.reshape(pair_count)[:, None], 0.0), axis=0)
    grads_picked = lax.dot_general(
        dispatch, grad_out, contract_first, preferred_element_type=jnp.float32
    )
    send_grads = (
        (weight_slot[:, None] * grads_picked)
        .astype(jnp.bfloat16)
        .reshape(groups, local_count * capacity, width)
    )
    packed = jnp.concatenate([w_gate, w_up, w_down], axis=2)
    packed = jnp.transpose(packed, (1, 0, 2)).reshape(shard_d, local_count * 3 * ff_width)
    full = all_gather_dp(packed, n_dp).reshape(width, local_count * 3 * ff_width)
    full = jnp.transpose(full.reshape(width, local_count, 3 * ff_width), (1, 0, 2))
    gate_full = full[:, :, :ff_width]
    up_full = full[:, :, ff_width : 2 * ff_width]
    down_full = full[:, :, 2 * ff_width :]
    recv_rows = shift_send([send_rows[s] for s in range(groups)], groups, 1)
    recv_grads = shift_send([send_grads[s] for s in range(groups)], groups, 1)
    gate_w = gate_full[0]
    up_w = up_full[0]
    down_w = down_full[0]
    x_rows = jnp.concatenate(recv_rows, axis=0)
    g_rows = jnp.concatenate(recv_grads, axis=0)
    gate_pre, up_pre, hidden, expert_out = forward_rows(x_rows, gate_w, up_w, down_w)
    expert_out, g_rows = lax.optimization_barrier((expert_out, g_rows))
    pair_grad = backward_rows(g_rows, gate_pre, up_pre, gate_w, up_w, down_w)
    pieces = lax.dot_general(g_rows, hidden, contract_first, preferred_element_type=jnp.float32)
    block_rows = local_count * capacity
    out_blocks = [expert_out[s * block_rows : (s + 1) * block_rows] for s in range(groups)]
    grad_blocks = [pair_grad[s * block_rows : (s + 1) * block_rows] for s in range(groups)]
    back_out = jnp.concatenate(shift_send(out_blocks, groups, -1), axis=0)
    back_grad = jnp.concatenate(shift_send(grad_blocks, groups, -1), axis=0)
    output = None
    for choice in range(top_count):
        pick = hit3[:, choice, :].astype(jnp.bfloat16)
        part = routing[:, choice][:, None] * jnp.dot(
            pick, back_out, preferred_element_type=jnp.float32
        )
        output = part if output is None else output + part
    output = output.astype(jnp.bfloat16)
    gather_both = jnp.sum(hit3.astype(jnp.int32), axis=1).astype(jnp.bfloat16)
    token_grad = jnp.dot(
        gather_both, back_grad, preferred_element_type=jnp.float32
    ).astype(jnp.bfloat16)
    summed = reduce_scatter_dp(pieces.reshape(n_dp, shard_d, ff_width), n_dp)
    down_grad = (summed / n_dp).reshape(local_count, shard_d, ff_width)
    return (output, token_grad, down_grad)


def solution(mesh):
    return jax.shard_map(
        local,
        mesh=mesh,
        in_specs=(
            P(("dp", "expert"), None),
            P(("dp", "expert"), None),
            P(("dp", "expert"), None),
            P("expert", "dp", None),
            P("expert", "dp", None),
            P("expert", "dp", None),
            P(("dp", "expert"), None),
        ),
        out_specs=(P(("dp", "expert"), None), P(("dp", "expert"), None), P("expert", "dp", None)),
        check_vma=False,
    )
```

```python
import jax
import jax.numpy as jnp
from jax import lax
from jax.sharding import PartitionSpec as P

contract_last = (((1,), (1,)), ((), ()))
contract_first = (((0,), (0,)), ((), ()))


def forward_rows(row_data, gate_w, up_w, down_w):
    gate_pre = jnp.dot(row_data, gate_w, preferred_element_type=jnp.float32)
    up_pre = jnp.dot(row_data, up_w, preferred_element_type=jnp.float32)
    sigmoid_val = jax.nn.sigmoid(gate_pre)
    hidden = (gate_pre * sigmoid_val * up_pre).astype(jnp.bfloat16)
    expert_out = lax.dot_general(
        hidden, down_w, contract_last, preferred_element_type=jnp.float32
    ).astype(jnp.bfloat16)
    return (gate_pre, up_pre, hidden, expert_out)


def backward_rows(grad_rows, gate_pre, up_pre, gate_w, up_w, down_w):
    hidden_grad = jnp.dot(grad_rows, down_w, preferred_element_type=jnp.float32)
    sigmoid_val = jax.nn.sigmoid(gate_pre)
    slope_val = sigmoid_val * (1.0 + gate_pre * (1.0 - sigmoid_val))
    gate_grad = (hidden_grad * up_pre * slope_val).astype(jnp.bfloat16)
    up_grad = (hidden_grad * gate_pre * sigmoid_val).astype(jnp.bfloat16)
    summed = lax.dot_general(gate_grad, gate_w, contract_last, preferred_element_type=jnp.float32)
    summed = summed + lax.dot_general(
        up_grad, up_w, contract_last, preferred_element_type=jnp.float32
    )
    return summed.astype(jnp.bfloat16)


def shift_send(blocks, groups, sign):
    got = [blocks[0]]
    for step in range(1, groups):
        pairs = [(i, (i + sign * step) % groups) for i in range(groups)]
        got.append(lax.ppermute(blocks[step], "expert", pairs))
    return got


def all_gather_dp(block, n_dp):
    me = lax.axis_index("dp")
    bits = []
    bit = n_dp // 2
    while bit >= 1:
        bits.append(bit)
        bit //= 2
    if len(bits) >= 3:
        bits[0], bits[1] = bits[1], bits[0]
    work = block
    for bit in bits:
        recv = lax.ppermute(work, "dp", [(i, i ^ bit) for i in range(n_dp)])
        upper = (me // bit) % 2 == 1
        work = jnp.stack([jnp.where(upper, recv, work), jnp.where(upper, work, recv)], axis=0)
    axes = list(reversed(bits))
    perm = sorted(range(len(bits)), key=lambda a: -axes[a])
    work = jnp.transpose(work, perm + list(range(len(bits), work.ndim)))
    return work.reshape((n_dp,) + block.shape)


def reduce_scatter_dp(pieces, n_dp, hold=None):
    me = lax.axis_index("dp")
    work = pieces
    bit = 1
    while bit < n_dp:
        if bit == 2 and hold is not None:
            work, hold = lax.optimization_barrier((work, hold))
        halves = work.reshape((work.shape[0] // 2, 2) + work.shape[1:])
        mine = (me // bit) % 2
        keep = jnp.take(halves, mine, axis=1)
        give = jnp.take(halves, 1 - mine, axis=1)
        pairs = [(i, i ^ bit) for i in range(n_dp)]
        work = keep + lax.ppermute(give, "dp", pairs)
        bit *= 2
    return work[0], hold


def local(tokens, expert_ids, routing, w_gate, w_up, w_down, grad_out):
    tok_rows, width = tokens.shape
    groups = lax.axis_size("expert")
    n_dp = lax.axis_size("dp")
    me = lax.axis_index("expert")
    local_count = w_gate.shape[0]
    ff_width = w_gate.shape[2]
    shard_d = w_gate.shape[1]
    experts_all = local_count * groups
    top_count = expert_ids.shape[1]
    capacity = 3 * tok_rows * top_count // (2 * experts_all)
    pair_count = tok_rows * top_count
    chosen = expert_ids.reshape(pair_count)
    home = chosen // local_count
    rotated = ((home - me) % groups) * local_count + chosen % local_count
    onehot = (rotated[:, None] == jnp.arange(experts_all, dtype=jnp.int32)[None, :]).astype(
        jnp.bfloat16
    )
    earlier = (
        jnp.arange(pair_count, dtype=jnp.int32)[:, None]
        > jnp.arange(pair_count, dtype=jnp.int32)[None, :]
    ).astype(jnp.bfloat16)
    before = jnp.dot(earlier, onehot, preferred_element_type=jnp.float32)
    slot_index = jnp.sum(before * onehot.astype(jnp.float32), axis=1).astype(jnp.int32)
    flat_index = rotated * capacity + slot_index
    slots = experts_all * capacity
    hit = flat_index[:, None] == jnp.arange(slots, dtype=jnp.int32)[None, :]
    hit3 = hit.reshape(tok_rows, top_count, slots)
    dispatch = jnp.any(hit3, axis=1).astype(jnp.bfloat16)
    send_rows = (
        lax.dot_general(dispatch, tokens, contract_first, preferred_element_type=jnp.float32)
        .astype(jnp.bfloat16)
        .reshape(groups, local_count * capacity, width)
    )
    weight_slot = jnp.sum(jnp.where(hit, routing.reshape(pair_count)[:, None], 0.0), axis=0)
    grads_picked = lax.dot_general(
        dispatch, grad_out, contract_first, preferred_element_type=jnp.float32
    )
    send_grads = (
        (weight_slot[:, None] * grads_picked)
        .astype(jnp.bfloat16)
        .reshape(groups, local_count * capacity, width)
    )
    packed = jnp.concatenate([w_gate, w_up, w_down], axis=2)
    packed = jnp.transpose(packed, (1, 0, 2)).reshape(shard_d, local_count * 3 * ff_width)
    full = all_gather_dp(packed, n_dp).reshape(width, local_count * 3 * ff_width)
    full = jnp.transpose(full.reshape(width, local_count, 3 * ff_width), (1, 0, 2))
    gate_full = full[:, :, :ff_width]
    up_full = full[:, :, ff_width : 2 * ff_width]
    down_full = full[:, :, 2 * ff_width :]
    recv_rows = shift_send([send_rows[s] for s in range(groups)], groups, 1)
    recv_grads = shift_send([send_grads[s] for s in range(groups)], groups, 1)
    gate_w = gate_full[0]
    up_w = up_full[0]
    down_w = down_full[0]
    x_rows = jnp.concatenate(recv_rows, axis=0)
    g_rows = jnp.concatenate(recv_grads, axis=0)
    gate_pre, up_pre, hidden, expert_out = forward_rows(x_rows, gate_w, up_w, down_w)
    pair_grad = backward_rows(g_rows, gate_pre, up_pre, gate_w, up_w, down_w)
    pieces = lax.dot_general(g_rows, hidden, contract_first, preferred_element_type=jnp.float32)
    block_rows = local_count * capacity
    out_blocks = [expert_out[s * block_rows : (s + 1) * block_rows] for s in range(groups)]
    summed, pair_grad = reduce_scatter_dp(pieces.reshape(n_dp, shard_d, ff_width), n_dp, pair_grad)
    grad_blocks = [pair_grad[s * block_rows : (s + 1) * block_rows] for s in range(groups)]
    back_out = jnp.concatenate(shift_send(out_blocks, groups, -1), axis=0)
    back_grad = jnp.concatenate(shift_send(grad_blocks, groups, -1), axis=0)
    output = None
    for choice in range(top_count):
        pick = hit3[:, choice, :].astype(jnp.bfloat16)
        part = routing[:, choice][:, None] * jnp.dot(
            pick, back_out, preferred_element_type=jnp.float32
        )
        output = part if output is None else output + part
    output = output.astype(jnp.bfloat16)
    gather_both = jnp.sum(hit3.astype(jnp.int32), axis=1).astype(jnp.bfloat16)
    token_grad = jnp.dot(
        gather_both, back_grad, preferred_element_type=jnp.float32
    ).astype(jnp.bfloat16)
    down_grad = (summed / n_dp).reshape(local_count, shard_d, ff_width)
    return (output, token_grad, down_grad)


def solution(mesh):
    return jax.shard_map(
        local,
        mesh=mesh,
        in_specs=(
            P(("dp", "expert"), None),
            P(("dp", "expert"), None),
            P(("dp", "expert"), None),
            P("expert", "dp", None),
            P("expert", "dp", None),
            P("expert", "dp", None),
            P(("dp", "expert"), None),
        ),
        out_specs=(P(("dp", "expert"), None), P(("dp", "expert"), None), P("expert", "dp", None)),
        check_vma=False,
    )
```

```python
import jax
import jax.numpy as jnp
from jax import lax
from jax.sharding import PartitionSpec as P

contract_last = (((1,), (1,)), ((), ()))
contract_first = (((0,), (0,)), ((), ()))


def forward_rows(row_data, gate_w, up_w, down_w):
    gate_pre = jnp.dot(row_data, gate_w, preferred_element_type=jnp.float32)
    up_pre = jnp.dot(row_data, up_w, preferred_element_type=jnp.float32)
    sigmoid_val = jax.nn.sigmoid(gate_pre)
    hidden = (gate_pre * sigmoid_val * up_pre).astype(jnp.bfloat16)
    expert_out = lax.dot_general(
        hidden, down_w, contract_last, preferred_element_type=jnp.float32
    ).astype(jnp.bfloat16)
    return (gate_pre, up_pre, hidden, expert_out)


def backward_rows(grad_rows, gate_pre, up_pre, gate_w, up_w, down_w):
    hidden_grad = jnp.dot(grad_rows, down_w, preferred_element_type=jnp.float32)
    sigmoid_val = jax.nn.sigmoid(gate_pre)
    slope_val = sigmoid_val * (1.0 + gate_pre * (1.0 - sigmoid_val))
    gate_grad = (hidden_grad * up_pre * slope_val).astype(jnp.bfloat16)
    up_grad = (hidden_grad * gate_pre * sigmoid_val).astype(jnp.bfloat16)
    summed = lax.dot_general(gate_grad, gate_w, contract_last, preferred_element_type=jnp.float32)
    summed = summed + lax.dot_general(
        up_grad, up_w, contract_last, preferred_element_type=jnp.float32
    )
    return summed.astype(jnp.bfloat16)


def shift_send(blocks, groups, sign):
    got = [blocks[0]]
    for step in range(1, groups):
        pairs = [(i, (i + sign * step) % groups) for i in range(groups)]
        got.append(lax.ppermute(blocks[step], "expert", pairs))
    return got


def all_gather_dp(block, n_dp):
    me = lax.axis_index("dp")
    bits = []
    bit = n_dp // 2
    while bit >= 1:
        bits.append(bit)
        bit //= 2
    if len(bits) >= 3:
        bits[0], bits[1] = bits[1], bits[0]
    work = block
    for bit in bits:
        recv = lax.ppermute(work, "dp", [(i, i ^ bit) for i in range(n_dp)])
        upper = (me // bit) % 2 == 1
        work = jnp.stack([jnp.where(upper, recv, work), jnp.where(upper, work, recv)], axis=0)
    axes = list(reversed(bits))
    perm = sorted(range(len(bits)), key=lambda a: -axes[a])
    work = jnp.transpose(work, perm + list(range(len(bits), work.ndim)))
    return work.reshape((n_dp,) + block.shape)


def reduce_scatter_dp(pieces, n_dp):
    me = lax.axis_index("dp")
    axes = []
    bit = n_dp // 2
    while bit >= 1:
        axes.append(bit)
        bit //= 2
    order = sorted(axes)
    if len(order) >= 3:
        order = order[:1] + order[1:][::-1]
    work = pieces.reshape((2,) * len(axes) + pieces.shape[1:])
    for bit in order:
        ax = axes.index(bit)
        mine = (me // bit) % 2
        keep = jnp.take(work, mine, axis=ax)
        give = jnp.take(work, 1 - mine, axis=ax)
        work = keep + lax.ppermute(give, "dp", [(i, i ^ bit) for i in range(n_dp)])
        axes.pop(ax)
    return work


def local(tokens, expert_ids, routing, w_gate, w_up, w_down, grad_out):
    tok_rows, width = tokens.shape
    groups = lax.axis_size("expert")
    n_dp = lax.axis_size("dp")
    me = lax.axis_index("expert")
    local_count = w_gate.shape[0]
    ff_width = w_gate.shape[2]
    shard_d = w_gate.shape[1]
    experts_all = local_count * groups
    top_count = expert_ids.shape[1]
    capacity = 3 * tok_rows * top_count // (2 * experts_all)
    pair_count = tok_rows * top_count
    chosen = expert_ids.reshape(pair_count)
    home = chosen // local_count
    rotated = ((home - me) % groups) * local_count + chosen % local_count
    onehot = (rotated[:, None] == jnp.arange(experts_all, dtype=jnp.int32)[None, :]).astype(
        jnp.bfloat16
    )
    earlier = (
        jnp.arange(pair_count, dtype=jnp.int32)[:, None]
        > jnp.arange(pair_count, dtype=jnp.int32)[None, :]
    ).astype(jnp.bfloat16)
    before = jnp.dot(earlier, onehot, preferred_element_type=jnp.float32)
    slot_index = jnp.sum(before * onehot.astype(jnp.float32), axis=1).astype(jnp.int32)
    flat_index = rotated * capacity + slot_index
    slots = experts_all * capacity
    hit = flat_index[:, None] == jnp.arange(slots, dtype=jnp.int32)[None, :]
    hit3 = hit.reshape(tok_rows, top_count, slots)
    dispatch = jnp.any(hit3, axis=1).astype(jnp.bfloat16)
    send_rows = (
        lax.dot_general(dispatch, tokens, contract_first, preferred_element_type=jnp.float32)
        .astype(jnp.bfloat16)
        .reshape(groups, local_count * capacity, width)
    )
    weight_slot = jnp.sum(jnp.where(hit, routing.reshape(pair_count)[:, None], 0.0), axis=0)
    grads_picked = lax.dot_general(
        dispatch, grad_out, contract_first, preferred_element_type=jnp.float32
    )
    send_grads = (
        (weight_slot[:, None] * grads_picked)
        .astype(jnp.bfloat16)
        .reshape(groups, local_count * capacity, width)
    )
    packed = jnp.concatenate([w_gate, w_up, w_down], axis=2)
    packed = jnp.transpose(packed, (1, 0, 2)).reshape(shard_d, local_count * 3 * ff_width)
    full = all_gather_dp(packed, n_dp).reshape(width, local_count * 3 * ff_width)
    full = jnp.transpose(full.reshape(width, local_count, 3 * ff_width), (1, 0, 2))
    gate_full = full[:, :, :ff_width]
    up_full = full[:, :, ff_width : 2 * ff_width]
    down_full = full[:, :, 2 * ff_width :]
    recv_rows = shift_send([send_rows[s] for s in range(groups)], groups, 1)
    recv_grads = shift_send([send_grads[s] for s in range(groups)], groups, 1)
    gate_w = gate_full[0]
    up_w = up_full[0]
    down_w = down_full[0]
    x_rows = jnp.concatenate(recv_rows, axis=0)
    g_rows = jnp.concatenate(recv_grads, axis=0)
    gate_pre, up_pre, hidden, expert_out = forward_rows(x_rows, gate_w, up_w, down_w)
    pair_grad = backward_rows(g_rows, gate_pre, up_pre, gate_w, up_w, down_w)
    pieces = lax.dot_general(g_rows, hidden, contract_first, preferred_element_type=jnp.float32)
    block_rows = local_count * capacity
    out_blocks = [expert_out[s * block_rows : (s + 1) * block_rows] for s in range(groups)]
    grad_blocks = [pair_grad[s * block_rows : (s + 1) * block_rows] for s in range(groups)]
    back_out = jnp.concatenate(shift_send(out_blocks, groups, -1), axis=0)
    back_grad = jnp.concatenate(shift_send(grad_blocks, groups, -1), axis=0)
    output = None
    for choice in range(top_count):
        pick = hit3[:, choice, :].astype(jnp.bfloat16)
        part = routing[:, choice][:, None] * jnp.dot(
            pick, back_out, preferred_element_type=jnp.float32
        )
        output = part if output is None else output + part
    output = output.astype(jnp.bfloat16)
    gather_both = jnp.sum(hit3.astype(jnp.int32), axis=1).astype(jnp.bfloat16)
    token_grad = jnp.dot(
        gather_both, back_grad, preferred_element_type=jnp.float32
    ).astype(jnp.bfloat16)
    summed = reduce_scatter_dp(pieces.reshape(n_dp, shard_d, ff_width), n_dp)
    down_grad = (summed / n_dp).reshape(local_count, shard_d, ff_width)
    return (output, token_grad, down_grad)


def solution(mesh):
    return jax.shard_map(
        local,
        mesh=mesh,
        in_specs=(
            P(("dp", "expert"), None),
            P(("dp", "expert"), None),
            P(("dp", "expert"), None),
            P("expert", "dp", None),
            P("expert", "dp", None),
            P("expert", "dp", None),
            P(("dp", "expert"), None),
        ),
        out_specs=(P(("dp", "expert"), None), P(("dp", "expert"), None), P("expert", "dp", None)),
        check_vma=False,
    )
```

```python
import jax
import jax.numpy as jnp
from jax import lax
from jax.sharding import PartitionSpec as P

contract_last = (((1,), (1,)), ((), ()))
contract_first = (((0,), (0,)), ((), ()))


def forward_rows(row_data, gate_up_w, down_w):
    ff_width = down_w.shape[1]
    both = jnp.dot(row_data, gate_up_w, preferred_element_type=jnp.float32)
    gate_pre = both[:, :ff_width]
    up_pre = both[:, ff_width:]
    sigmoid_val = jax.nn.sigmoid(gate_pre)
    hidden = (gate_pre * sigmoid_val * up_pre).astype(jnp.bfloat16)
    expert_out = lax.dot_general(
        hidden, down_w, contract_last, preferred_element_type=jnp.float32
    ).astype(jnp.bfloat16)
    return (gate_pre, up_pre, hidden, expert_out)


def backward_rows(grad_rows, gate_pre, up_pre, gate_up_w, down_w):
    hidden_grad = jnp.dot(grad_rows, down_w, preferred_element_type=jnp.float32)
    sigmoid_val = jax.nn.sigmoid(gate_pre)
    slope_val = sigmoid_val * (1.0 + gate_pre * (1.0 - sigmoid_val))
    gate_grad = (hidden_grad * up_pre * slope_val).astype(jnp.bfloat16)
    up_grad = (hidden_grad * gate_pre * sigmoid_val).astype(jnp.bfloat16)
    summed = lax.dot_general(
        jnp.concatenate([gate_grad, up_grad], axis=1),
        gate_up_w,
        contract_last,
        preferred_element_type=jnp.float32,
    )
    return summed.astype(jnp.bfloat16)


def shift_send(blocks, groups, sign):
    got = [blocks[0]]
    for step in range(1, groups):
        pairs = [(i, (i + sign * step) % groups) for i in range(groups)]
        got.append(lax.ppermute(blocks[step], "expert", pairs))
    return got


def all_gather_dp(block, n_dp):
    me = lax.axis_index("dp")
    bits = []
    bit = n_dp // 2
    while bit >= 1:
        bits.append(bit)
        bit //= 2
    if len(bits) >= 3:
        bits[0], bits[1] = bits[1], bits[0]
    work = block
    for bit in bits:
        recv = lax.ppermute(work, "dp", [(i, i ^ bit) for i in range(n_dp)])
        upper = (me // bit) % 2 == 1
        work = jnp.stack([jnp.where(upper, recv, work), jnp.where(upper, work, recv)], axis=0)
    axes = list(reversed(bits))
    perm = sorted(range(len(bits)), key=lambda a: -axes[a])
    work = jnp.transpose(work, perm + list(range(len(bits), work.ndim)))
    return work.reshape((n_dp,) + block.shape)


def reduce_scatter_dp(pieces, n_dp):
    me = lax.axis_index("dp")
    axes = []
    bit = n_dp // 2
    while bit >= 1:
        axes.append(bit)
        bit //= 2
    order = sorted(axes)
    if len(order) >= 3:
        order = order[:1] + order[1:][::-1]
    work = pieces.reshape((2,) * len(axes) + pieces.shape[1:])
    for bit in order:
        ax = axes.index(bit)
        mine = (me // bit) % 2
        keep = jnp.take(work, mine, axis=ax)
        give = jnp.take(work, 1 - mine, axis=ax)
        work = keep + lax.ppermute(give, "dp", [(i, i ^ bit) for i in range(n_dp)])
        axes.pop(ax)
    return work


def local(tokens, expert_ids, routing, w_gate, w_up, w_down, grad_out):
    tok_rows, width = tokens.shape
    groups = lax.axis_size("expert")
    n_dp = lax.axis_size("dp")
    me = lax.axis_index("expert")
    local_count = w_gate.shape[0]
    ff_width = w_gate.shape[2]
    shard_d = w_gate.shape[1]
    experts_all = local_count * groups
    top_count = expert_ids.shape[1]
    capacity = 3 * tok_rows * top_count // (2 * experts_all)
    pair_count = tok_rows * top_count
    chosen = expert_ids.reshape(pair_count)
    home = chosen // local_count
    rotated = ((home - me) % groups) * local_count + chosen % local_count
    onehot = (rotated[:, None] == jnp.arange(experts_all, dtype=jnp.int32)[None, :]).astype(
        jnp.bfloat16
    )
    earlier = (
        jnp.arange(pair_count, dtype=jnp.int32)[:, None]
        > jnp.arange(pair_count, dtype=jnp.int32)[None, :]
    ).astype(jnp.bfloat16)
    before = jnp.dot(earlier, onehot, preferred_element_type=jnp.float32)
    slot_index = jnp.sum(before * onehot.astype(jnp.float32), axis=1).astype(jnp.int32)
    flat_index = rotated * capacity + slot_index
    slots = experts_all * capacity
    hit = flat_index[:, None] == jnp.arange(slots, dtype=jnp.int32)[None, :]
    hit3 = hit.reshape(tok_rows, top_count, slots)
    dispatch = jnp.any(hit3, axis=1).astype(jnp.bfloat16)
    send_rows = (
        lax.dot_general(dispatch, tokens, contract_first, preferred_element_type=jnp.float32)
        .astype(jnp.bfloat16)
        .reshape(groups, local_count * capacity, width)
    )
    weight_slot = jnp.sum(jnp.where(hit, routing.reshape(pair_count)[:, None], 0.0), axis=0)
    grads_picked = lax.dot_general(
        dispatch, grad_out, contract_first, preferred_element_type=jnp.float32
    )
    send_grads = (
        (weight_slot[:, None] * grads_picked)
        .astype(jnp.bfloat16)
        .reshape(groups, local_count * capacity, width)
    )
    packed = jnp.concatenate([w_gate, w_up, w_down], axis=2)
    packed = jnp.transpose(packed, (1, 0, 2)).reshape(shard_d, local_count * 3 * ff_width)
    full = all_gather_dp(packed, n_dp).reshape(width, local_count * 3 * ff_width)
    full = jnp.transpose(full.reshape(width, local_count, 3 * ff_width), (1, 0, 2))
    down_full = full[:, :, 2 * ff_width :]
    recv_rows = shift_send([send_rows[s] for s in range(groups)], groups, 1)
    recv_grads = shift_send([send_grads[s] for s in range(groups)], groups, 1)
    gate_up_w = full[0, :, : 2 * ff_width]
    down_w = down_full[0]
    x_rows = jnp.concatenate(recv_rows, axis=0)
    g_rows = jnp.concatenate(recv_grads, axis=0)
    gate_pre, up_pre, hidden, expert_out = forward_rows(x_rows, gate_up_w, down_w)
    pair_grad = backward_rows(g_rows, gate_pre, up_pre, gate_up_w, down_w)
    pieces = lax.dot_general(g_rows, hidden, contract_first, preferred_element_type=jnp.float32)
    block_rows = local_count * capacity
    out_blocks = [expert_out[s * block_rows : (s + 1) * block_rows] for s in range(groups)]
    grad_blocks = [pair_grad[s * block_rows : (s + 1) * block_rows] for s in range(groups)]
    back_out = jnp.concatenate(shift_send(out_blocks, groups, -1), axis=0)
    back_grad = jnp.concatenate(shift_send(grad_blocks, groups, -1), axis=0)
    output = None
    for choice in range(top_count):
        pick = hit3[:, choice, :].astype(jnp.bfloat16)
        part = routing[:, choice][:, None] * jnp.dot(
            pick, back_out, preferred_element_type=jnp.float32
        )
        output = part if output is None else output + part
    output = output.astype(jnp.bfloat16)
    gather_both = jnp.sum(hit3.astype(jnp.int32), axis=1).astype(jnp.bfloat16)
    token_grad = jnp.dot(
        gather_both, back_grad, preferred_element_type=jnp.float32
    ).astype(jnp.bfloat16)
    summed = reduce_scatter_dp(pieces.reshape(n_dp, shard_d, ff_width), n_dp)
    down_grad = (summed / n_dp).reshape(local_count, shard_d, ff_width)
    return (output, token_grad, down_grad)


def solution(mesh):
    return jax.shard_map(
        local,
        mesh=mesh,
        in_specs=(
            P(("dp", "expert"), None),
            P(("dp", "expert"), None),
            P(("dp", "expert"), None),
            P("expert", "dp", None),
            P("expert", "dp", None),
            P("expert", "dp", None),
            P(("dp", "expert"), None),
        ),
        out_specs=(P(("dp", "expert"), None), P(("dp", "expert"), None), P("expert", "dp", None)),
        check_vma=False,
    )
```
